128 devices in a mesh: mx: 16 (over y, z_lo, core), my: 8 (over z_hi, x).
Axes of the slice: x: 4, y: 4, z: 4 (z_hi: 2, z_lo: 2; z = z_hi * 2 + z_lo), core: 2. Of those that a mesh axis runs over, the one named last changes fastest.
Arguments:
- documents: bfloat16 [131072, 768], P(('mx', 'my')), may hold values from -12 to 12
- owner_tile: int32 [131072, 1], P(('mx', 'my')), may hold values from 0 to 127; in each aligned block of 1024 rows (0 to 1023, 1024 to 2047, ...) at most 16 rows name the same one
- unit_in_tile: int32 [131072], P(('mx', 'my')), may hold values from 0 to 4095
- codebook: bfloat16 [1024, 512, 768], P('mx', 'my'), may hold values from -6 to 6
Outputs:
- new_codebook: bfloat16 [1024, 512, 768], P('mx', 'my')
The draws below stay inside these ranges and needn't reach their ends.
Inputs may be any that keep to these rules, and one draw needn't show every extreme that they name: `owner_tile`: among the rows of one device no tile is named by more than 16 documents, and in every draw some tile is named by exactly 16 rows of some device.
All inputs are finite; a program needn't handle non-finite values.
Results may differ from the reference program's by a relative error of at most 0.001.
Values may be sent and summed in bfloat16 or wider, within the bound.
No kernel may reach another device: no remote copies, remote signals or barrier semaphores. Data moves between devices by JAX's collectives and lax.ppermute only.
A program may use at most 256 MiB of HBM per device.

```python
import math
import jax
import jax.numpy as jnp
import numpy as np
from jax import lax

E = 768
TR = 64
TC = 64
RADIUS = 8
DOC_DEV = 1024
TILES = 128
CAP = 16
MR = 1024
MC = 512
DOCS = 131072
N_MY = 8


def with_ends(values, own_key, smallest, high):
    longest = values.shape.index(max(values.shape))
    spots = []
    for shift in (0, 1):
        where = [jax.random.randint(jax.random.fold_in(own_key, axis), (), 0, length) for axis, length in enumerate(values.shape)]
        where[longest] = (where[longest] + shift) % values.shape[longest]
        spots.append(tuple(where))
    return values.at[spots[0]].set(smallest).at[spots[1]].set(high)


def block_scale(rng, dims, shards, least, top_value):
    factor_of = 1.0
    for dim, shards_of in shards:
        steps = jax.random.uniform(jax.random.fold_in(jax.random.fold_in(rng, 6), dim), (shards_of,), jnp.float32, least / len(shards), top_value / len(shards))
        factor_of = factor_of * jnp.repeat(jnp.exp(steps), dims[dim] // shards_of).reshape((-1,) + (1,) * (len(dims) - 1 - dim))
    return factor_of


def assign_block(key, own, number, rows, amount, top, reach, skew):
    ranking = jax.random.permutation(key, amount)
    packed, usual = portions_of(amount, rows * top, reach, skew, True), portions_of(amount, rows * top, reach, skew, False)
    places = jnp.arange(amount)

    def named(sizes, offset_by):
        used = int((sizes > 0).sum())
        fixed = max(1, used // 4)
        passed = fixed + (places - fixed + offset_by * (used - fixed)) % max(1, amount - fixed)
        return jnp.zeros((amount,), jnp.int32).at[ranking[jnp.where(places < fixed, places, passed)]].set(jnp.asarray(sizes, jnp.int32))

    sizes = jnp.where(number % 4 == 0, named(packed, number // 4), named(usual, number - number // 4 - 1))
    mixed = jax.random.permutation(jax.random.fold_in(own, 3), amount)
    giver, taker = mixed[0:amount // 2 * 2:2], mixed[1:amount // 2 * 2:2]
    room = jnp.minimum(sizes[giver] - 1, reach - sizes[taker]) // 2
    room = jnp.where((giver == ranking[0]) | (taker == ranking[0]) | (sizes[taker] == 0), 0, jnp.maximum(room, 0))
    passed = jax.random.randint(jax.random.fold_in(own, 4), (amount // 2,), 0, 1 << 20) % (room + 1)
    sizes = sizes.at[giver].add(-passed).at[taker].add(passed)
    labels = jnp.searchsorted(jnp.cumsum(sizes), jnp.arange(rows * top), side="right").astype(jnp.int32)
    grid = labels.reshape(top, rows).T
    grid = grid[jax.random.permutation(jax.random.fold_in(own, 1), rows)]
    offset_by = jax.random.randint(jax.random.fold_in(own, 2), (rows, 1), 0, top)
    return jnp.take_along_axis(grid, (jnp.arange(top)[None, :] + offset_by) % top, axis=1)


def portions_of(number_of, total, most, lean, full):
    weights = [(1 << 20) // math.isqrt(standing ** lean) + 1 for standing in range(1, number_of + 1)]
    largest = most if full else min(most, max(-(-total // number_of), total * weights[0] // sum(weights)))
    least = 1 if total - largest >= number_of - 1 else 0
    holding, surplus = [largest] + [least] * (number_of - 1), total - largest - least * (number_of - 1)
    while surplus > 0:
        candidates = [i for i in range(1, number_of) if holding[i] < largest] or [i for i in range(1, number_of) if holding[i] < most]
        mass, left = sum([weights[i] for i in candidates]), surplus
        for i in candidates:
            addition = min(most - holding[i], max(1, left * weights[i] // mass), surplus)
            holding[i] = holding[i] + addition
            surplus = surplus - addition
    return np.array(holding)


def gaussian(key, shape, spread, bound, shards=(), dtype=jnp.bfloat16):
    loudness = block_scale(key, shape, shards, -0.22, 0.18) if shards else 1.0
    drawn = jax.random.normal(key, shape, jnp.float32) * spread * loudness
    return jnp.minimum(jnp.maximum(drawn, -bound), bound).astype(dtype)


def setup_inputs(seed: int = 0) -> dict:
    splits = jax.random.split(jax.random.key(seed), 5)
    documents = gaussian(splits[0], (DOCS, E), 2.0, 12.0, ((0, 128),))
    owner_tile_keys = jax.random.split(jax.random.fold_in(splits[1], 1), DOCS // DOC_DEV)
    owner_tile_turns = jax.random.permutation(jax.random.fold_in(splits[1], 3), DOCS // DOC_DEV)
    owner_tile = jax.vmap(lambda own, number: assign_block(jax.random.fold_in(splits[1], 2), own, number, DOC_DEV, TILES, 1, CAP, 2))(owner_tile_keys, owner_tile_turns).reshape((DOCS, 1))
    unit_in_tile = with_ends(jax.random.randint(splits[2], (DOCS,), 0, TR * TC), jax.random.fold_in(splits[2], 1), 0, (TR * TC) - 1).astype(jnp.int32)
    codebook = gaussian(splits[3], (MR, MC, E), 1.0, 6.0, ((0, 16), (1, 8)))
    return {"documents": documents, "owner_tile": owner_tile, "unit_in_tile": unit_in_tile, "codebook": codebook}


def smooth_along(values_in, axis_dim, extent):
    weights = [math.exp(-2.0 * shift_k * shift_k / RADIUS ** 2) for shift_k in range(-RADIUS, RADIUS + 1)]
    pads = [(0, 0)] * values_in.ndim
    pads[axis_dim] = (RADIUS, RADIUS)
    padded = jnp.pad(values_in, pads)
    result = weights[0] * lax.slice_in_dim(padded, 0, extent, axis=axis_dim)
    for place in range(1, 2 * RADIUS + 1):
        result = result + weights[place] * lax.slice_in_dim(padded, place, place + extent, axis=axis_dim)
    return result


def smooth_map(values_in):
    return smooth_along(smooth_along(values_in, 0, MR), 1, MC)


def reference(documents, owner_tile, unit_in_tile, codebook):
    tile_of = owner_tile[:, 0]
    win_row = (tile_of // N_MY) * TR + unit_in_tile // TC
    win_col = (tile_of % N_MY) * TC + unit_in_tile % TC
    flat_unit = (win_row * MC + win_col).astype(jnp.int32)
    hits = jax.ops.segment_sum(jnp.ones((DOCS,), jnp.float32), flat_unit, MR * MC).reshape(MR, MC)
    smooth_hits = smooth_map(hits)
    block_width = 128 if E % 128 == 0 else E
    block_count = E // block_width
    docs_blocks = documents.reshape(DOCS, block_count, block_width).transpose(1, 0, 2)
    code_blocks = codebook.reshape(MR, MC, block_count, block_width).transpose(2, 0, 1, 3)

    def one_block(pieces):
        doc_part, code_part = pieces
        numerator = jax.ops.segment_sum(doc_part.astype(jnp.float32), flat_unit, MR * MC).reshape(MR, MC, block_width)
        smoothed = smooth_map(numerator)
        updated = (smoothed + 8.0 * code_part.astype(jnp.float32)) / (smooth_hits[:, :, None] + 8.0)
        return updated.astype(jnp.bfloat16)

    blocks_out = lax.map(one_block, (docs_blocks, code_blocks))
    return blocks_out.transpose(1, 2, 0, 3).reshape(MR, MC, E)
```

```python
import math

import jax
import jax.numpy as jnp
import numpy as np
from jax import lax
from jax.experimental import pallas as pl
from jax.sharding import PartitionSpec as P

RADIUS = 8
HI = lax.Precision.HIGHEST


def band_matrix(out_len):
    ext = out_len + 2 * RADIUS
    mat = np.zeros((out_len, ext), np.float32)
    for r in range(out_len):
        for k in range(-RADIUS, RADIUS + 1):
            mat[r, r + k + RADIUS] = math.exp(-2.0 * k * k / RADIUS**2)
    return mat


def accumulate_kernel(ids_ref, docs_ref, num_ref, hits_ref):
    block, rows = num_ref.shape[0], ids_ref.shape[1]
    first = pl.program_id(0) * block
    units = first + lax.broadcasted_iota(jnp.int32, (block, rows), 0)
    one_hot = (units == ids_ref[...]).astype(jnp.bfloat16)
    num_ref[...] = jnp.dot(one_hot, docs_ref[...], preferred_element_type=jnp.float32)
    ones = jnp.ones((rows, hits_ref.shape[1]), jnp.bfloat16)
    hits_ref[...] = jnp.dot(one_hot, ones, preferred_element_type=jnp.float32)


def accumulate(ids, docs, unit_total):
    rows, feature = docs.shape
    block = 512
    return pl.pallas_call(
        accumulate_kernel,
        grid=(unit_total // block,),
        in_specs=[
            pl.BlockSpec((1, rows), lambda j: (0, 0)),
            pl.BlockSpec((rows, feature), lambda j: (0, 0)),
        ],
        out_specs=[
            pl.BlockSpec((block, feature), lambda j: (j, 0)),
            pl.BlockSpec((block, 128), lambda j: (j, 0)),
        ],
        out_shape=[
            jax.ShapeDtypeStruct((unit_total, feature), jnp.float32),
            jax.ShapeDtypeStruct((unit_total, 128), jnp.float32),
        ],
    )(ids.reshape(1, rows), docs)


def halo(x, axis, dim):
    devices, length = lax.axis_size(axis), x.shape[dim]
    up = [(i, i + 1) for i in range(devices - 1)]
    down = [(j, i) for i, j in up]
    last = lax.slice_in_dim(x, length - RADIUS, length, axis=dim)
    leading = lax.slice_in_dim(x, 0, RADIUS, axis=dim)
    before = lax.ppermute(last, axis, up)
    after = lax.ppermute(leading, axis, down)
    return jnp.concatenate([before, x, after], axis=dim)


def on_device(documents, owner_tile, unit_in_tile, codebook):
    rows_mx = lax.axis_size("mx")
    cols_my = lax.axis_size("my")
    tile_total = rows_mx * cols_my
    rows_tile, cols_tile, feature = codebook.shape
    doc_count = documents.shape[0]
    capacity = max(2, 2 * doc_count // tile_total)
    depth = capacity + 1
    target = owner_tile[:, 0]
    tile_hits = (target[:, None] == jnp.arange(tile_total, dtype=jnp.int32)[None, :]).astype(
        jnp.int32
    )
    earlier = jnp.cumsum(tile_hits, axis=0) - tile_hits
    slot_pos = jnp.sum(earlier * tile_hits, axis=1)
    unit_row = unit_in_tile // cols_tile
    unit_col = unit_in_tile % cols_tile
    send_place = target * depth + slot_pos
    outgoing = jnp.zeros((tile_total * depth, feature), jnp.bfloat16).at[send_place].set(documents)
    unit_mark = jnp.stack([unit_row, unit_col], axis=1).astype(jnp.bfloat16)
    slot_marks = (
        jnp.full((tile_total * capacity, 2), -1.0, jnp.bfloat16)
        .at[target * capacity + slot_pos]
        .set(unit_mark)
        .reshape(tile_total, 1, 2 * capacity)
    )
    outgoing = outgoing.reshape(tile_total, depth, feature)
    outgoing = lax.dynamic_update_slice(outgoing, slot_marks, (0, capacity, 0))
    got = lax.all_to_all(outgoing, ("mx", "my"), split_axis=0, concat_axis=0, tiled=True)
    marks_in = got[:, capacity, : 2 * capacity].reshape(tile_total, capacity, 2)
    mark_row = marks_in[:, :, 0].astype(jnp.int32)
    mark_col = marks_in[:, :, 1].astype(jnp.int32)
    unit_ids = jnp.where(mark_row < 0, -1, mark_row * cols_tile + mark_col)
    unit_ids = jnp.concatenate(
        [unit_ids, jnp.full((tile_total, 1), -1, jnp.int32)], axis=1
    ).reshape(-1)
    unit_total = rows_tile * cols_tile
    numerator, counter = accumulate(unit_ids, got.reshape(-1, feature), unit_total)
    numerator = numerator.reshape(rows_tile, cols_tile, feature)
    counter = counter[:, 0].reshape(rows_tile, cols_tile)

    g_rows = jnp.asarray(band_matrix(rows_tile))
    g_cols = jnp.asarray(band_matrix(cols_tile))
    ext_num = halo(numerator, "mx", 0)
    ext_hits = halo(counter, "mx", 0)
    row_num = jnp.einsum("rk,kce->rce", g_rows, ext_num, precision=HI)
    row_hits = jnp.einsum("rk,kc->rc", g_rows, ext_hits, precision=HI)
    ext_num = halo(row_num, "my", 1)
    ext_hits = halo(row_hits, "my", 1)
    smooth_num = jnp.einsum("ck,rke->rce", g_cols, ext_num, precision=HI)
    smooth_hits = jnp.einsum("ck,rk->rc", g_cols, ext_hits, precision=HI)
    updated = (smooth_num + 8.0 * codebook.astype(jnp.float32)) / (smooth_hits[:, :, None] + 8.0)
    return updated.astype(jnp.bfloat16)


def solution(mesh):
    return jax.shard_map(
        on_device,
        mesh=mesh,
        in_specs=(
            P(("mx", "my"), None),
            P(("mx", "my"), None),
            P(("mx", "my")),
            P("mx", "my", None),
        ),
        out_specs=P("mx", "my", None),
        check_vma=False,
    )
```

```python
import math

import jax
import jax.numpy as jnp
import numpy as np
from jax import lax
from jax.experimental import pallas as pl
from jax.sharding import PartitionSpec as P

RADIUS = 8
HI = lax.Precision.HIGH


def band_matrix(out_len):
    ext = out_len + 2 * RADIUS
    mat = np.zeros((out_len, ext), np.float32)
    for r in range(out_len):
        for k in range(-RADIUS, RADIUS + 1):
            mat[r, r + k + RADIUS] = math.exp(-2.0 * k * k / RADIUS**2)
    return mat


def accumulate_kernel(ids_ref, docs_ref, num_ref, hits_ref):
    block, rows = num_ref.shape[0], ids_ref.shape[1]
    feature = num_ref.shape[1]
    first = pl.program_id(0) * block
    units = first + lax.broadcasted_iota(jnp.int32, (block, rows), 0)
    one_hot = (units == ids_ref[...]).astype(jnp.bfloat16)
    sums = jnp.dot(one_hot, docs_ref[...], preferred_element_type=jnp.float32)
    num_ref[...] = sums[:, :feature]
    hits_ref[...] = sums[:, feature:]


def accumulate(ids, docs, unit_total, feature):
    rows, width = docs.shape
    block = 512
    return pl.pallas_call(
        accumulate_kernel,
        grid=(unit_total // block,),
        in_specs=[
            pl.BlockSpec((1, rows), lambda j: (0, 0)),
            pl.BlockSpec((rows, width), lambda j: (0, 0)),
        ],
        out_specs=[
            pl.BlockSpec((block, feature), lambda j: (j, 0)),
            pl.BlockSpec((block, width - feature), lambda j: (j, 0)),
        ],
        out_shape=[
            jax.ShapeDtypeStruct((unit_total, feature), jnp.float32),
            jax.ShapeDtypeStruct((unit_total, width - feature), jnp.float32),
        ],
    )(ids.reshape(1, rows), docs)


def halo(x, axis, dim):
    devices, length = lax.axis_size(axis), x.shape[dim]
    up = [(i, i + 1) for i in range(devices - 1)]
    down = [(j, i) for i, j in up]
    last = lax.slice_in_dim(x, length - RADIUS, length, axis=dim)
    leading = lax.slice_in_dim(x, 0, RADIUS, axis=dim)
    before = lax.ppermute(last, axis, up)
    after = lax.ppermute(leading, axis, down)
    return jnp.concatenate([before, x, after], axis=dim)


def on_device(documents, owner_tile, unit_in_tile, codebook):
    rows_mx = lax.axis_size("mx")
    cols_my = lax.axis_size("my")
    tile_total = rows_mx * cols_my
    rows_tile, cols_tile, feature = codebook.shape
    doc_count = documents.shape[0]
    capacity = max(2, 2 * doc_count // tile_total)
    target = owner_tile[:, 0]
    tile_hits = (target[:, None] == jnp.arange(tile_total, dtype=jnp.int32)[None, :]).astype(
        jnp.int32
    )
    earlier = jnp.cumsum(tile_hits, axis=0) - tile_hits
    slot_pos = jnp.sum(earlier * tile_hits, axis=1)
    unit_row = unit_in_tile // cols_tile
    unit_col = unit_in_tile % cols_tile
    extra = jnp.zeros((doc_count, 128), jnp.bfloat16)
    extra = extra.at[:, 0].set(unit_row.astype(jnp.bfloat16))
    extra = extra.at[:, 1].set(unit_col.astype(jnp.bfloat16))
    extra = extra.at[:, 2].set(1.0)
    rows_out = jnp.concatenate([documents, extra], axis=1)
    width = feature + 128
    send_place = target * capacity + slot_pos
    outgoing = jnp.zeros((tile_total * capacity, width), jnp.bfloat16).at[send_place].set(rows_out)
    got = lax.all_to_all(
        outgoing.reshape(tile_total, capacity, width),
        ("mx", "my"),
        split_axis=0,
        concat_axis=0,
        tiled=True,
    ).reshape(-1, width)
    mark_row = got[:, feature].astype(jnp.int32)
    mark_col = got[:, feature + 1].astype(jnp.int32)
    unit_ids = jnp.where(got[:, feature + 2] > 0.5, mark_col * rows_tile + mark_row, -1)
    unit_total = rows_tile * cols_tile
    numerator, counter = accumulate(unit_ids, got, unit_total, feature)
    num_cm = numerator.reshape(cols_tile, rows_tile, feature)
    hits_cm = counter[:, 2].reshape(cols_tile, rows_tile)

    g_rows = jnp.asarray(band_matrix(rows_tile))
    g_cols = jnp.asarray(band_matrix(cols_tile))
    ext_num = halo(num_cm, "mx", 1)
    ext_hits = halo(hits_cm, "mx", 1)
    row_num = jnp.einsum("rk,cke->cre", g_rows, ext_num, precision=HI)
    row_hits = jnp.einsum("rk,ck->cr", g_rows, ext_hits, precision=HI)
    ext_num = halo(row_num, "my", 0)
    ext_hits = halo(row_hits, "my", 0)
    smooth_num = jnp.einsum("ck,kre->rce", g_cols, ext_num, precision=HI)
    smooth_hits = jnp.einsum("ck,kr->rc", g_cols, ext_hits, precision=HI)
    updated = (smooth_num + 8.0 * codebook.astype(jnp.float32)) / (smooth_hits[:, :, None] + 8.0)
    return updated.astype(jnp.bfloat16)


def solution(mesh):
    return jax.shard_map(
        on_device,
        mesh=mesh,
        in_specs=(
            P(("mx", "my"), None),
            P(("mx", "my"), None),
            P(("mx", "my")),
            P("mx", "my", None),
        ),
        out_specs=P("mx", "my", None),
        check_vma=False,
    )
```

```python
import math

import jax
import jax.numpy as jnp
import numpy as np
from jax import lax
from jax.experimental import pallas as pl
from jax.sharding import PartitionSpec as P

RADIUS = 8
HI = lax.Precision.HIGH


def band_matrix(out_len):
    ext = out_len + 2 * RADIUS
    mat = np.zeros((out_len, ext), np.float32)
    for r in range(out_len):
        for k in range(-RADIUS, RADIUS + 1):
            mat[r, r + k + RADIUS] = math.exp(-2.0 * k * k / RADIUS**2)
    return mat


def accumulate(ids, docs, unit_of, blocks, feature):
    rows, width = docs.shape
    block = 512

    def kernel(ids_ref, docs_ref, num_ref, hits_ref):
        place = pl.program_id(0) * block + lax.broadcasted_iota(jnp.int32, (block, rows), 0)
        units = unit_of(place)
        one_hot = (units == ids_ref[...]).astype(jnp.bfloat16)
        sums = jnp.dot(one_hot, docs_ref[...], preferred_element_type=jnp.float32)
        num_ref[...] = sums[:, :feature]
        hits_ref[...] = sums[:, feature:]

    return pl.pallas_call(
        kernel,
        grid=(blocks,),
        in_specs=[
            pl.BlockSpec((1, rows), lambda j: (0, 0)),
            pl.BlockSpec((rows, width), lambda j: (0, 0)),
        ],
        out_specs=[
            pl.BlockSpec((block, feature), lambda j: (j, 0)),
            pl.BlockSpec((block, width - feature), lambda j: (j, 0)),
        ],
        out_shape=[
            jax.ShapeDtypeStruct((blocks * block, feature), jnp.float32),
            jax.ShapeDtypeStruct((blocks * block, width - feature), jnp.float32),
        ],
    )(ids.reshape(1, rows), docs)


def exchange(lead, last, axis):
    devices = lax.axis_size(axis)
    up = [(i, i + 1) for i in range(devices - 1)]
    down = [(j, i) for i, j in up]
    return lax.ppermute(last, axis, up), lax.ppermute(lead, axis, down)


def on_device(documents, owner_tile, unit_in_tile, codebook):
    rows_mx = lax.axis_size("mx")
    cols_my = lax.axis_size("my")
    tile_total = rows_mx * cols_my
    rows_tile, cols_tile, feature = codebook.shape
    doc_count = documents.shape[0]
    capacity = max(2, 2 * doc_count // tile_total)
    target = owner_tile[:, 0]
    tile_hits = (target[:, None] == jnp.arange(tile_total, dtype=jnp.int32)[None, :]).astype(
        jnp.int32
    )
    earlier = jnp.cumsum(tile_hits, axis=0) - tile_hits
    slot_pos = jnp.sum(earlier * tile_hits, axis=1)
    unit_row = unit_in_tile // cols_tile
    unit_col = unit_in_tile % cols_tile
    extra = jnp.zeros((doc_count, 128), jnp.bfloat16)
    extra = extra.at[:, 0].set(unit_row.astype(jnp.bfloat16))
    extra = extra.at[:, 1].set(unit_col.astype(jnp.bfloat16))
    extra = extra.at[:, 2].set(1.0)
    rows_out = jnp.concatenate([documents, extra], axis=1)
    width = feature + 128
    send_place = target * capacity + slot_pos
    outgoing = jnp.zeros((tile_total * capacity, width), jnp.bfloat16).at[send_place].set(rows_out)
    got = lax.all_to_all(
        outgoing.reshape(tile_total, capacity, width),
        ("mx", "my"),
        split_axis=0,
        concat_axis=0,
        tiled=True,
    ).reshape(-1, width)
    mark_row = got[:, feature].astype(jnp.int32)
    mark_col = got[:, feature + 1].astype(jnp.int32)
    unit_ids = jnp.where(got[:, feature + 2] > 0.5, mark_row * cols_tile + mark_col, -1)
    inner = cols_tile - 2 * RADIUS
    band_blocks = RADIUS * rows_tile // 512
    inner_blocks = inner * rows_tile // 512

    def band_unit(offset):
        return lambda m: (m // RADIUS) * cols_tile + offset + m % RADIUS

    num_l, cnt_l = accumulate(unit_ids, got, band_unit(0), band_blocks, feature)
    num_r, cnt_r = accumulate(unit_ids, got, band_unit(cols_tile - RADIUS), band_blocks, feature)
    band_shape = (rows_tile, RADIUS, feature)
    num_l, num_r = num_l.reshape(band_shape), num_r.reshape(band_shape)
    hits_l = cnt_l[:, 2].reshape(rows_tile, RADIUS)
    hits_r = cnt_r[:, 2].reshape(rows_tile, RADIUS)
    from_left, from_right = exchange(num_l, num_r, "my")
    hits_from_left, hits_from_right = exchange(hits_l, hits_r, "my")
    num_i, cnt_i = accumulate(
        unit_ids, got, lambda m: (m // inner) * cols_tile + RADIUS + m % inner, inner_blocks, feature
    )
    num_i = num_i.reshape(rows_tile, inner, feature)
    hits_i = cnt_i[:, 2].reshape(rows_tile, inner)

    g_rows = jnp.asarray(band_matrix(rows_tile))
    g_cols = jnp.asarray(band_matrix(cols_tile))
    ext_num = jnp.concatenate([from_left, num_l, num_i, num_r, from_right], axis=1)
    ext_hits = jnp.concatenate([hits_from_left, hits_l, hits_i, hits_r, hits_from_right], axis=1)
    col_num = jnp.einsum("ck,rke->rce", g_cols, ext_num, precision=HI)
    col_hits = jnp.einsum("ck,rk->rc", g_cols, ext_hits, precision=HI)
    above, below = exchange(col_num[:RADIUS], col_num[rows_tile - RADIUS :], "mx")
    hits_above, hits_below = exchange(col_hits[:RADIUS], col_hits[rows_tile - RADIUS :], "mx")
    ext_num = jnp.concatenate([above, col_num, below], axis=0)
    ext_hits = jnp.concatenate([hits_above, col_hits, hits_below], axis=0)
    smooth_num = jnp.einsum("rk,kce->rce", g_rows, ext_num, precision=HI)
    smooth_hits = jnp.einsum("rk,kc->rc", g_rows, ext_hits, precision=HI)
    updated = (smooth_num + 8.0 * codebook.astype(jnp.float32)) / (smooth_hits[:, :, None] + 8.0)
    return updated.astype(jnp.bfloat16)


def solution(mesh):
    return jax.shard_map(
        on_device,
        mesh=mesh,
        in_specs=(
            P(("mx", "my"), None),
            P(("mx", "my"), None),
            P(("mx", "my")),
            P("mx", "my", None),
        ),
        out_specs=P("mx", "my", None),
        check_vma=False,
    )
```

```python
import math

import jax
import jax.numpy as jnp
import numpy as np
from jax import lax
from jax.experimental import pallas as pl
from jax.experimental.pallas import tpu as pltpu
from jax.sharding import PartitionSpec as P

RADIUS = 8
HI = lax.Precision.HIGH


def band_matrix(out_len):
    ext = out_len + 2 * RADIUS
    mat = np.zeros((out_len, ext), np.float32)
    for r in range(out_len):
        for k in range(-RADIUS, RADIUS + 1):
            mat[r, r + k + RADIUS] = math.exp(-2.0 * k * k / RADIUS**2)
    return mat


def accumulate(ids, docs, unit_of, blocks, feature):
    rows, width = docs.shape
    block = 512

    def kernel(ids_ref, docs_ref, num_ref, hits_ref):
        place = pl.program_id(0) * block + lax.broadcasted_iota(jnp.int32, (block, rows), 0)
        units = unit_of(place)
        one_hot = (units == ids_ref[...]).astype(jnp.bfloat16)
        sums = jnp.dot(one_hot, docs_ref[...], preferred_element_type=jnp.float32)
        num_ref[...] = sums[:, :feature]
        hits_ref[...] = sums[:, feature:]

    return pl.pallas_call(
        kernel,
        grid=(blocks,),
        in_specs=[
            pl.BlockSpec((1, rows), lambda j: (0, 0)),
            pl.BlockSpec((rows, width), lambda j: (0, 0)),
        ],
        out_specs=[
            pl.BlockSpec((block, feature), lambda j: (j, 0)),
            pl.BlockSpec((block, width - feature), lambda j: (j, 0)),
        ],
        out_shape=[
            jax.ShapeDtypeStruct((blocks * block, feature), jnp.float32),
            jax.ShapeDtypeStruct((blocks * block, width - feature), jnp.float32),
        ],
    )(ids.reshape(1, rows), docs)


def finish(above, middle, below, codebook, inv):
    rows, cols, feature = middle.shape
    lanes = 128
    taps = [math.exp(-2.0 * k * k / RADIUS**2) for k in range(RADIUS + 1)]

    def kernel(above_ref, mid_ref, below_ref, cb_ref, inv_ref, out_ref, ext_ref):
        ext_ref[0:RADIUS] = above_ref[...]
        ext_ref[RADIUS : RADIUS + rows] = mid_ref[...]
        ext_ref[RADIUS + rows :] = below_ref[...]

        def body(r, carry):
            centre = r + RADIUS
            acc = taps[0] * ext_ref[centre]
            for k in range(1, RADIUS + 1):
                acc = acc + taps[k] * (ext_ref[centre - k] + ext_ref[centre + k])
            upd = (acc + 8.0 * cb_ref[r].astype(jnp.float32)) * inv_ref[r]
            out_ref[r] = upd.astype(out_ref.dtype)
            return carry

        lax.fori_loop(0, rows, body, 0, unroll=2)

    halo_spec = pl.BlockSpec((RADIUS, cols, lanes), lambda j: (0, 0, j))
    slab_spec = pl.BlockSpec((rows, cols, lanes), lambda j: (0, 0, j))
    return pl.pallas_call(
        kernel,
        grid=(feature // lanes,),
        in_specs=[
            halo_spec,
            slab_spec,
            halo_spec,
            slab_spec,
            pl.BlockSpec((rows, cols, 1), lambda j: (0, 0, 0)),
        ],
        out_specs=slab_spec,
        out_shape=jax.ShapeDtypeStruct(codebook.shape, codebook.dtype),
        scratch_shapes=[pltpu.VMEM((rows + 2 * RADIUS, cols, lanes), jnp.float32)],
    )(above, middle, below, codebook, inv)


def exchange(lead, last, axis):
    devices = lax.axis_size(axis)
    up = [(i, i + 1) for i in range(devices - 1)]
    down = [(j, i) for i, j in up]
    return lax.ppermute(last, axis, up), lax.ppermute(lead, axis, down)


def on_device(documents, owner_tile, unit_in_tile, codebook):
    rows_mx = lax.axis_size("mx")
    cols_my = lax.axis_size("my")
    tile_total = rows_mx * cols_my
    rows_tile, cols_tile, feature = codebook.shape
    doc_count = documents.shape[0]
    capacity = max(2, 2 * doc_count // tile_total)
    target = owner_tile[:, 0]
    tile_hits = (target[:, None] == jnp.arange(tile_total, dtype=jnp.int32)[None, :]).astype(
        jnp.int32
    )
    earlier = jnp.cumsum(tile_hits, axis=0) - tile_hits
    slot_pos = jnp.sum(earlier * tile_hits, axis=1)
    unit_row = unit_in_tile // cols_tile
    unit_col = unit_in_tile % cols_tile
    extra = jnp.zeros((doc_count, 128), jnp.bfloat16)
    extra = extra.at[:, 0].set(unit_row.astype(jnp.bfloat16))
    extra = extra.at[:, 1].set(unit_col.astype(jnp.bfloat16))
    extra = extra.at[:, 2].set(1.0)
    rows_out = jnp.concatenate([documents, extra], axis=1)
    width = feature + 128
    send_place = target * capacity + slot_pos
    outgoing = jnp.zeros((tile_total * capacity, width), jnp.bfloat16).at[send_place].set(rows_out)
    got = lax.all_to_all(
        outgoing.reshape(tile_total, capacity, width),
        ("mx", "my"),
        split_axis=0,
        concat_axis=0,
        tiled=True,
    ).reshape(-1, width)
    mark_row = got[:, feature].astype(jnp.int32)
    mark_col = got[:, feature + 1].astype(jnp.int32)
    unit_ids = jnp.where(got[:, feature + 2] > 0.5, mark_row * cols_tile + mark_col, -1)
    numerator, counter = accumulate(
        unit_ids, got, lambda m: m, rows_tile * cols_tile // 512, feature
    )
    numerator = numerator.reshape(rows_tile, cols_tile, feature)
    counter = counter[:, 2].reshape(rows_tile, cols_tile)

    g_rows = jnp.asarray(band_matrix(rows_tile))
    g_cols = jnp.asarray(band_matrix(cols_tile))
    last = cols_tile - RADIUS
    from_left, from_right = exchange(numerator[:, :RADIUS], numerator[:, last:], "my")
    hits_left, hits_right = exchange(counter[:, :RADIUS], counter[:, last:], "my")
    ext_num = jnp.concatenate([from_left, numerator, from_right], axis=1)
    ext_hits = jnp.concatenate([hits_left, counter, hits_right], axis=1)
    col_num = jnp.einsum("ck,rke->rce", g_cols, ext_num, precision=HI)
    col_hits = jnp.einsum("ck,rk->rc", g_cols, ext_hits, precision=HI)
    last = rows_tile - RADIUS
    above, below = exchange(col_num[:RADIUS], col_num[last:], "mx")
    hits_above, hits_below = exchange(col_hits[:RADIUS], col_hits[last:], "mx")
    ext_hits = jnp.concatenate([hits_above, col_hits, hits_below], axis=0)
    smooth_hits = jnp.einsum("rk,kc->rc", g_rows, ext_hits, precision=HI)
    inv = (1.0 / (smooth_hits + 8.0))[:, :, None]
    return finish(above, col_num, below, codebook, inv)


def solution(mesh):
    return jax.shard_map(
        on_device,
        mesh=mesh,
        in_specs=(
            P(("mx", "my"), None),
            P(("mx", "my"), None),
            P(("mx", "my")),
            P("mx", "my", None),
        ),
        out_specs=P("mx", "my", None),
        check_vma=False,
    )
```

```python
import math

import jax
import jax.numpy as jnp
import numpy as np
from jax import lax
from jax.experimental import pallas as pl
from jax.experimental.pallas import tpu as pltpu
from jax.sharding import PartitionSpec as P

RADIUS = 8
HI = lax.Precision.HIGH


def band_matrix(out_len):
    ext = out_len + 2 * RADIUS
    mat = np.zeros((out_len, ext), np.float32)
    for r in range(out_len):
        for k in range(-RADIUS, RADIUS + 1):
            mat[r, r + k + RADIUS] = math.exp(-2.0 * k * k / RADIUS**2)
    return mat


def accumulate(ids, docs, unit_of, blocks, feature):
    rows, width = docs.shape
    block = 512

    def kernel(ids_ref, docs_ref, num_ref, hits_ref):
        place = pl.program_id(0) * block + lax.broadcasted_iota(jnp.int32, (block, rows), 0)
        units = unit_of(place)
        one_hot = (units == ids_ref[...]).astype(jnp.bfloat16)
        sums = jnp.dot(one_hot, docs_ref[...], preferred_element_type=jnp.float32)
        num_ref[...] = sums[:, :feature]
        hits_ref[...] = sums[:, feature:]

    return pl.pallas_call(
        kernel,
        grid=(blocks,),
        in_specs=[
            pl.BlockSpec((1, rows), lambda j: (0, 0)),
            pl.BlockSpec((rows, width), lambda j: (0, 0)),
        ],
        out_specs=[
            pl.BlockSpec((block, feature), lambda j: (j, 0)),
            pl.BlockSpec((block, width - feature), lambda j: (j, 0)),
        ],
        out_shape=[
            jax.ShapeDtypeStruct((blocks * block, feature), jnp.float32),
            jax.ShapeDtypeStruct((blocks * block, width - feature), jnp.float32),
        ],
    )(ids.reshape(1, rows), docs)


def finish_inner(middle, codebook, inv):
    rows, cols, feature = middle.shape
    lanes = 128

    def kernel(mid_ref, cb_ref, inv_ref, out_ref):
        ext = mid_ref
        taps = [math.exp(-2.0 * k * k / RADIUS**2) for k in range(RADIUS + 1)]

        def body(r, carry):
            acc = taps[0] * ext[r]
            for k in range(1, RADIUS + 1):
                acc = acc + taps[k] * (ext[r - k] + ext[r + k])
            upd = (acc + 8.0 * cb_ref[r].astype(jnp.float32)) * inv_ref[r]
            out_ref[r] = upd.astype(out_ref.dtype)
            return carry

        lax.fori_loop(RADIUS, rows - RADIUS, body, 0, unroll=2)

    slab_spec = pl.BlockSpec((rows, cols, lanes), lambda j: (0, 0, j))
    return pl.pallas_call(
        kernel,
        grid=(feature // lanes,),
        in_specs=[slab_spec, slab_spec, pl.BlockSpec((rows, cols, 1), lambda j: (0, 0, 0))],
        out_specs=slab_spec,
        out_shape=jax.ShapeDtypeStruct(codebook.shape, codebook.dtype),
    )(middle, codebook, inv)


def finish_edges(above, middle, below, codebook, inv, partial):
    rows, cols, feature = middle.shape
    lanes = 128
    near = 2 * RADIUS
    last_edge = rows // RADIUS - 1
    taps = [math.exp(-2.0 * k * k / RADIUS**2) for k in range(RADIUS + 1)]

    def kernel(above_ref, mid_ref, below_ref, cb_ref, inv_ref, prev_ref, out_ref, ext_ref):
        del prev_ref
        side = pl.program_id(0)

        @pl.when(side == 0)
        def _():
            ext_ref[0:RADIUS] = above_ref[...]
            ext_ref[RADIUS:] = mid_ref[...]

        @pl.when(side == 1)
        def _():
            ext_ref[0:near] = mid_ref[...]
            ext_ref[near:] = below_ref[...]

        def body(r, carry):
            centre = r + RADIUS
            acc = taps[0] * ext_ref[centre]
            for k in range(1, RADIUS + 1):
                acc = acc + taps[k] * (ext_ref[centre - k] + ext_ref[centre + k])
            upd = (acc + 8.0 * cb_ref[r].astype(jnp.float32)) * inv_ref[r]
            out_ref[r] = upd.astype(out_ref.dtype)
            return carry

        lax.fori_loop(0, RADIUS, body, 0, unroll=2)

    halo_spec = pl.BlockSpec((RADIUS, cols, lanes), lambda i, j: (0, 0, j))
    edge_spec = pl.BlockSpec((RADIUS, cols, lanes), lambda i, j: (i * last_edge, 0, j))
    return pl.pallas_call(
        kernel,
        grid=(2, feature // lanes),
        in_specs=[
            halo_spec,
            pl.BlockSpec((near, cols, lanes), lambda i, j: (i * (rows // near - 1), 0, j)),
            halo_spec,
            edge_spec,
            pl.BlockSpec((RADIUS, cols, 1), lambda i, j: (i * last_edge, 0, 0)),
            pl.BlockSpec(memory_space=pl.ANY),
        ],
        out_specs=edge_spec,
        out_shape=jax.ShapeDtypeStruct(codebook.shape, codebook.dtype),
        scratch_shapes=[pltpu.VMEM((near + RADIUS, cols, lanes), jnp.float32)],
        input_output_aliases={5: 0},
    )(above, middle, below, codebook, inv, partial)


def exchange(lead, last, axis):
    devices = lax.axis_size(axis)
    up = [(i, i + 1) for i in range(devices - 1)]
    down = [(j, i) for i, j in up]
    return lax.ppermute(last, axis, up), lax.ppermute(lead, axis, down)


def on_device(documents, owner_tile, unit_in_tile, codebook):
    rows_mx = lax.axis_size("mx")
    cols_my = lax.axis_size("my")
    tile_total = rows_mx * cols_my
    rows_tile, cols_tile, feature = codebook.shape
    doc_count = documents.shape[0]
    capacity = max(2, 2 * doc_count // tile_total)
    target = owner_tile[:, 0]
    tile_hits = (target[:, None] == jnp.arange(tile_total, dtype=jnp.int32)[None, :]).astype(
        jnp.int32
    )
    earlier = jnp.cumsum(tile_hits, axis=0) - tile_hits
    slot_pos = jnp.sum(earlier * tile_hits, axis=1)
    unit_row = unit_in_tile // cols_tile
    unit_col = unit_in_tile % cols_tile
    extra = jnp.zeros((doc_count, 128), jnp.bfloat16)
    extra = extra.at[:, 0].set(unit_row.astype(jnp.bfloat16))
    extra = extra.at[:, 1].set(unit_col.astype(jnp.bfloat16))
    extra = extra.at[:, 2].set(1.0)
    rows_out = jnp.concatenate([documents, extra], axis=1)
    width = feature + 128
    send_place = target * capacity + slot_pos
    outgoing = jnp.zeros((tile_total * capacity, width), jnp.bfloat16).at[send_place].set(rows_out)
    got = lax.all_to_all(
        outgoing.reshape(tile_total, capacity, width),
        ("mx", "my"),
        split_axis=0,
        concat_axis=0,
        tiled=True,
    ).reshape(-1, width)
    mark_row = got[:, feature].astype(jnp.int32)
    mark_col = got[:, feature + 1].astype(jnp.int32)
    unit_ids = jnp.where(got[:, feature + 2] > 0.5, mark_row * cols_tile + mark_col, -1)
    numerator, counter = accumulate(
        unit_ids, got, lambda m: m, rows_tile * cols_tile // 512, feature
    )
    numerator = numerator.reshape(rows_tile, cols_tile, feature)
    counter = counter[:, 2].reshape(rows_tile, cols_tile)

    g_rows = jnp.asarray(band_matrix(rows_tile))
    g_cols = jnp.asarray(band_matrix(cols_tile))
    last = cols_tile - RADIUS
    from_left, from_right = exchange(numerator[:, :RADIUS], numerator[:, last:], "my")
    hits_left, hits_right = exchange(counter[:, :RADIUS], counter[:, last:], "my")
    ext_num = jnp.concatenate([from_left, numerator, from_right], axis=1)
    ext_hits = jnp.concatenate([hits_left, counter, hits_right], axis=1)
    col_num = jnp.einsum("ck,rke->rce", g_cols, ext_num, precision=HI)
    col_hits = jnp.einsum("ck,rk->rc", g_cols, ext_hits, precision=HI)
    last = rows_tile - RADIUS
    above, below = exchange(col_num[:RADIUS], col_num[last:], "mx")
    hits_above, hits_below = exchange(col_hits[:RADIUS], col_hits[last:], "mx")
    ext_hits = jnp.concatenate([hits_above, col_hits, hits_below], axis=0)
    smooth_hits = jnp.einsum("rk,kc->rc", g_rows, ext_hits, precision=HI)
    inv = (1.0 / (smooth_hits + 8.0))[:, :, None]
    partial = finish_inner(col_num, codebook, inv)
    return finish_edges(above, col_num, below, codebook, inv, partial)


def solution(mesh):
    return jax.shard_map(
        on_device,
        mesh=mesh,
        in_specs=(
            P(("mx", "my"), None),
            P(("mx", "my"), None),
            P(("mx", "my")),
            P("mx", "my", None),
        ),
        out_specs=P("mx", "my", None),
        check_vma=False,
    )
```

```python
import math

import jax
import jax.numpy as jnp
import numpy as np
from jax import lax
from jax.experimental import pallas as pl
from jax.experimental.pallas import tpu as pltpu
from jax.sharding import PartitionSpec as P

RADIUS = 8
HI = lax.Precision.HIGH


def band_matrix(out_len):
    ext = out_len + 2 * RADIUS
    mat = np.zeros((out_len, ext), np.float32)
    for r in range(out_len):
        for k in range(-RADIUS, RADIUS + 1):
            mat[r, r + k + RADIUS] = math.exp(-2.0 * k * k / RADIUS**2)
    return mat


def accumulate(ids, docs, unit_of, blocks, feature):
    rows, width = docs.shape
    block = 512

    def kernel(ids_ref, docs_ref, num_ref, hits_ref):
        place = pl.program_id(0) * block + lax.broadcasted_iota(jnp.int32, (block, rows), 0)
        units = unit_of(place)
        one_hot = (units == ids_ref[...]).astype(jnp.bfloat16)
        sums = jnp.dot(one_hot, docs_ref[...], preferred_element_type=jnp.float32)
        num_ref[...] = sums[:, :feature]
        hits_ref[...] = sums[:, feature:]

    return pl.pallas_call(
        kernel,
        grid=(blocks,),
        in_specs=[
            pl.BlockSpec((1, rows), lambda j: (0, 0)),
            pl.BlockSpec((rows, width), lambda j: (0, 0)),
        ],
        out_specs=[
            pl.BlockSpec((block, feature), lambda j: (j, 0)),
            pl.BlockSpec((block, width - feature), lambda j: (j, 0)),
        ],
        out_shape=[
            jax.ShapeDtypeStruct((blocks * block, feature), jnp.float32),
            jax.ShapeDtypeStruct((blocks * block, width - feature), jnp.float32),
        ],
    )(ids.reshape(1, rows), docs)


def finish_inner(middle, codebook, inv):
    rows, cols, feature = middle.shape
    lanes = 128

    def kernel(mid_ref, cb_ref, inv_ref, out_ref):
        ext = mid_ref
        taps = [math.exp(-2.0 * k * k / RADIUS**2) for k in range(RADIUS + 1)]

        def body(r, carry):
            acc = taps[0] * ext[r]
            for k in range(1, RADIUS + 1):
                acc = acc + taps[k] * (ext[r - k] + ext[r + k])
            upd = (acc + 8.0 * cb_ref[r].astype(jnp.float32)) * inv_ref[r]
            out_ref[r] = upd.astype(out_ref.dtype)
            return carry

        lax.fori_loop(RADIUS, rows - RADIUS, body, 0, unroll=2)

    slab_spec = pl.BlockSpec((rows, cols, lanes), lambda j: (0, 0, j))
    return pl.pallas_call(
        kernel,
        grid=(feature // lanes,),
        in_specs=[slab_spec, slab_spec, pl.BlockSpec((rows, cols, 1), lambda j: (0, 0, 0))],
        out_specs=slab_spec,
        out_shape=jax.ShapeDtypeStruct(codebook.shape, codebook.dtype),
    )(middle, codebook, inv)


def finish_edges(above, middle, below, codebook, inv, partial):
    rows, cols, feature = middle.shape
    lanes = 128
    near = 2 * RADIUS
    last_edge = rows // RADIUS - 1
    taps = [math.exp(-2.0 * k * k / RADIUS**2) for k in range(RADIUS + 1)]

    def kernel(above_ref, mid_ref, below_ref, cb_ref, inv_ref, prev_ref, out_ref, ext_ref):
        del prev_ref
        side = pl.program_id(0)

        @pl.when(side == 0)
        def _():
            ext_ref[0:RADIUS] = above_ref[...]
            ext_ref[RADIUS:] = mid_ref[...]

        @pl.when(side == 1)
        def _():
            ext_ref[0:near] = mid_ref[...]
            ext_ref[near:] = below_ref[...]

        def body(r, carry):
            centre = r + RADIUS
            scale = inv_ref[r]
            for lane in range(0, feature, lanes):
                part = pl.ds(lane, lanes)
                acc = taps[0] * ext_ref[centre, :, part]
                for k in range(1, RADIUS + 1):
                    acc = acc + taps[k] * (ext_ref[centre - k, :, part] + ext_ref[centre + k, :, part])
                upd = (acc + 8.0 * cb_ref[r, :, part].astype(jnp.float32)) * scale
                out_ref[r, :, part] = upd.astype(out_ref.dtype)
            return carry

        lax.fori_loop(0, RADIUS, body, 0)

    halo_spec = pl.BlockSpec((RADIUS, cols, feature), lambda i: (0, 0, 0))
    edge_spec = pl.BlockSpec((RADIUS, cols, feature), lambda i: (i * last_edge, 0, 0))
    return pl.pallas_call(
        kernel,
        grid=(2,),
        in_specs=[
            halo_spec,
            pl.BlockSpec((near, cols, feature), lambda i: (i * (rows // near - 1), 0, 0)),
            halo_spec,
            edge_spec,
            pl.BlockSpec((RADIUS, cols, 1), lambda i: (i, 0, 0)),
            pl.BlockSpec(memory_space=pl.ANY),
        ],
        out_specs=edge_spec,
        out_shape=jax.ShapeDtypeStruct(codebook.shape, codebook.dtype),
        scratch_shapes=[pltpu.VMEM((near + RADIUS, cols, feature), jnp.float32)],
        input_output_aliases={5: 0},
    )(above, middle, below, codebook, inv, partial)


def exchange(lead, last, axis):
    devices = lax.axis_size(axis)
    up = [(i, i + 1) for i in range(devices - 1)]
    down = [(j, i) for i, j in up]
    return lax.ppermute(last, axis, up), lax.ppermute(lead, axis, down)


def on_device(documents, owner_tile, unit_in_tile, codebook):
    rows_mx = lax.axis_size("mx")
    cols_my = lax.axis_size("my")
    tile_total = rows_mx * cols_my
    rows_tile, cols_tile, feature = codebook.shape
    doc_count = documents.shape[0]
    capacity = max(2, 2 * doc_count // tile_total)
    target = owner_tile[:, 0]
    tile_hits = (target[:, None] == jnp.arange(tile_total, dtype=jnp.int32)[None, :]).astype(
        jnp.int32
    )
    earlier = jnp.cumsum(tile_hits, axis=0) - tile_hits
    slot_pos = jnp.sum(earlier * tile_hits, axis=1)
    unit_row = unit_in_tile // cols_tile
    unit_col = unit_in_tile % cols_tile
    extra = jnp.zeros((doc_count, 128), jnp.bfloat16)
    extra = extra.at[:, 0].set(unit_row.astype(jnp.bfloat16))
    extra = extra.at[:, 1].set(unit_col.astype(jnp.bfloat16))
    extra = extra.at[:, 2].set(1.0)
    rows_out = jnp.concatenate([documents, extra], axis=1)
    width = feature + 128
    send_place = target * capacity + slot_pos
    outgoing = jnp.zeros((tile_total * capacity, width), jnp.bfloat16).at[send_place].set(rows_out)
    got = lax.all_to_all(
        outgoing.reshape(tile_total, capacity, width),
        ("mx", "my"),
        split_axis=0,
        concat_axis=0,
        tiled=True,
    ).reshape(-1, width)
    mark_row = got[:, feature].astype(jnp.int32)
    mark_col = got[:, feature + 1].astype(jnp.int32)
    unit_ids = jnp.where(got[:, feature + 2] > 0.5, mark_row * cols_tile + mark_col, -1)
    numerator, counter = accumulate(
        unit_ids, got, lambda m: m, rows_tile * cols_tile // 512, feature
    )
    numerator = numerator.reshape(rows_tile, cols_tile, feature)
    counter = counter[:, 2].reshape(rows_tile, cols_tile)

    g_rows = jnp.asarray(band_matrix(rows_tile))
    g_cols = jnp.asarray(band_matrix(cols_tile))
    last = cols_tile - RADIUS
    from_left, from_right = exchange(numerator[:, :RADIUS], numerator[:, last:], "my")
    hits_left, hits_right = exchange(counter[:, :RADIUS], counter[:, last:], "my")
    ext_num = jnp.concatenate([from_left, numerator, from_right], axis=1)
    ext_hits = jnp.concatenate([hits_left, counter, hits_right], axis=1)
    col_num = jnp.einsum("ck,rke->rce", g_cols, ext_num, precision=HI)
    col_hits = jnp.einsum("ck,rk->rc", g_cols, ext_hits, precision=HI)
    last = rows_tile - RADIUS
    above, below = exchange(col_num[:RADIUS], col_num[last:], "mx")
    hits_above, hits_below = exchange(col_hits[:RADIUS], col_hits[last:], "mx")
    inner_hits = jnp.einsum("rk,kc->rc", g_rows[RADIUS:last, RADIUS : RADIUS + rows_tile], col_hits, precision=HI)
    inv_inner = 1.0 / (inner_hits + 8.0)
    inv = jnp.concatenate([jnp.zeros_like(inv_inner[:RADIUS]), inv_inner, jnp.zeros_like(inv_inner[:RADIUS])])
    inv = inv[:, :, None]
    edge_top = jnp.concatenate([hits_above, col_hits[: 2 * RADIUS]], axis=0)
    edge_bottom = jnp.concatenate([col_hits[last - RADIUS :], hits_below], axis=0)
    g_edge = g_rows[:RADIUS, : 3 * RADIUS]
    top_hits = jnp.einsum("rk,kc->rc", g_edge, edge_top, precision=HI)
    bottom_hits = jnp.einsum("rk,kc->rc", g_edge, edge_bottom, precision=HI)
    inv_edges = (1.0 / (jnp.concatenate([top_hits, bottom_hits], axis=0) + 8.0))[:, :, None]
    partial = finish_inner(col_num, codebook, inv)
    return finish_edges(above, col_num, below, codebook, inv_edges, partial)


def solution(mesh):
    return jax.shard_map(
        on_device,
        mesh=mesh,
        in_specs=(
            P(("mx", "my"), None),
            P(("mx", "my"), None),
            P(("mx", "my")),
            P("mx", "my", None),
        ),
        out_specs=P("mx", "my", None),
        check_vma=False,
    )
```

```python
import math

import jax
import jax.numpy as jnp
import numpy as np
from jax import lax
from jax.experimental import pallas as pl
from jax.experimental.pallas import tpu as pltpu
from jax.sharding import PartitionSpec as P

RADIUS = 8
HI = lax.Precision.HIGH


def band_matrix(out_len):
    ext = out_len + 2 * RADIUS
    mat = np.zeros((out_len, ext), np.float32)
    for r in range(out_len):
        for k in range(-RADIUS, RADIUS + 1):
            mat[r, r + k + RADIUS] = math.exp(-2.0 * k * k / RADIUS**2)
    return mat


def accumulate(ids, docs, unit_of, blocks, feature):
    rows, width = docs.shape
    block = 512

    def kernel(ids_ref, docs_ref, num_ref, hits_ref):
        place = pl.program_id(0) * block + lax.broadcasted_iota(jnp.int32, (block, rows), 0)
        units = unit_of(place)
        one_hot = (units == ids_ref[...]).astype(jnp.bfloat16)
        sums = jnp.dot(one_hot, docs_ref[...], preferred_element_type=jnp.float32)
        num_ref[...] = sums[:, :feature]
        hits_ref[...] = sums[:, feature:]

    return pl.pallas_call(
        kernel,
        grid=(blocks,),
        in_specs=[
            pl.BlockSpec((1, rows), lambda j: (0, 0)),
            pl.BlockSpec((rows, width), lambda j: (0, 0)),
        ],
        out_specs=[
            pl.BlockSpec((block, feature), lambda j: (j, 0)),
            pl.BlockSpec((block, width - feature), lambda j: (j, 0)),
        ],
        out_shape=[
            jax.ShapeDtypeStruct((blocks * block, feature), jnp.float32),
            jax.ShapeDtypeStruct((blocks * block, width - feature), jnp.float32),
        ],
    )(ids.reshape(1, rows), docs)


def finish_inner(middle, codebook, inv):
    rows, cols, feature = middle.shape
    lanes = 128

    def kernel(mid_ref, cb_ref, inv_ref, out_ref):
        ext = mid_ref
        taps = [math.exp(-2.0 * k * k / RADIUS**2) for k in range(RADIUS + 1)]

        def body(r, carry):
            acc = taps[0] * ext[r]
            for k in range(1, RADIUS + 1):
                acc = acc + taps[k] * (ext[r - k] + ext[r + k])
            upd = (acc + 8.0 * cb_ref[r].astype(jnp.float32)) * inv_ref[r]
            out_ref[r] = upd.astype(out_ref.dtype)
            return carry

        lax.fori_loop(RADIUS, rows - RADIUS, body, 0, unroll=2)

    slab_spec = pl.BlockSpec((rows, cols, lanes), lambda j: (0, 0, j))
    return pl.pallas_call(
        kernel,
        grid=(feature // lanes,),
        in_specs=[slab_spec, slab_spec, pl.BlockSpec((rows, cols, 1), lambda j: (0, 0, 0))],
        out_specs=slab_spec,
        out_shape=jax.ShapeDtypeStruct(codebook.shape, codebook.dtype),
    )(middle, codebook, inv)


def finish_edges(above, middle, below, codebook, inv, partial):
    rows, cols, feature = middle.shape
    lanes = 128
    near = 2 * RADIUS
    last_edge = rows // RADIUS - 1
    taps = [math.exp(-2.0 * k * k / RADIUS**2) for k in range(RADIUS + 1)]

    def kernel(above_ref, mid_ref, below_ref, cb_ref, inv_ref, prev_ref, out_ref, ext_ref):
        del prev_ref
        side = pl.program_id(0)

        @pl.when(side == 0)
        def _():
            ext_ref[0:RADIUS] = above_ref[...]
            ext_ref[RADIUS:] = mid_ref[...]

        @pl.when(side == 1)
        def _():
            ext_ref[0:near] = mid_ref[...]
            ext_ref[near:] = below_ref[...]

        def body(r, carry):
            centre = r + RADIUS
            scale = inv_ref[r]
            for lane in range(0, feature, lanes):
                part = pl.ds(lane, lanes)
                acc = taps[0] * ext_ref[centre, :, part]
                for k in range(1, RADIUS + 1):
                    acc = acc + taps[k] * (ext_ref[centre - k, :, part] + ext_ref[centre + k, :, part])
                upd = (acc + 8.0 * cb_ref[r, :, part].astype(jnp.float32)) * scale
                out_ref[r, :, part] = upd.astype(out_ref.dtype)
            return carry

        lax.fori_loop(0, RADIUS, body, 0)

    halo_spec = pl.BlockSpec((RADIUS, cols, feature), lambda i: (0, 0, 0))
    edge_spec = pl.BlockSpec((RADIUS, cols, feature), lambda i: (i * last_edge, 0, 0))
    return pl.pallas_call(
        kernel,
        grid=(2,),
        in_specs=[
            halo_spec,
            pl.BlockSpec((near, cols, feature), lambda i: (i * (rows // near - 1), 0, 0)),
            halo_spec,
            edge_spec,
            pl.BlockSpec((RADIUS, cols, 1), lambda i: (i, 0, 0)),
            pl.BlockSpec(memory_space=pl.ANY),
        ],
        out_specs=edge_spec,
        out_shape=jax.ShapeDtypeStruct(codebook.shape, codebook.dtype),
        scratch_shapes=[pltpu.VMEM((near + RADIUS, cols, feature), jnp.float32)],
        input_output_aliases={5: 0},
    )(above, middle, below, codebook, inv, partial)


def exchange(lead, last, axis):
    devices = lax.axis_size(axis)
    up = [(i, i + 1) for i in range(devices - 1)]
    down = [(j, i) for i, j in up]
    return lax.ppermute(last, axis, up), lax.ppermute(lead, axis, down)


def on_device(documents, owner_tile, unit_in_tile, codebook):
    rows_mx = lax.axis_size("mx")
    cols_my = lax.axis_size("my")
    tile_total = rows_mx * cols_my
    rows_tile, cols_tile, feature = codebook.shape
    doc_count = documents.shape[0]
    capacity = max(2, 2 * doc_count // tile_total)
    target = owner_tile[:, 0]
    tile_hits = (target[:, None] == jnp.arange(tile_total, dtype=jnp.int32)[None, :]).astype(
        jnp.int32
    )
    earlier = jnp.cumsum(tile_hits, axis=0) - tile_hits
    slot_pos = jnp.sum(earlier * tile_hits, axis=1)
    unit_row = unit_in_tile // cols_tile
    unit_col = unit_in_tile % cols_tile
    extra = jnp.zeros((doc_count, 128), jnp.bfloat16)
    extra = extra.at[:, 0].set(unit_row.astype(jnp.bfloat16))
    extra = extra.at[:, 1].set(unit_col.astype(jnp.bfloat16))
    extra = extra.at[:, 2].set(1.0)
    rows_out = jnp.concatenate([documents, extra], axis=1)
    width = feature + 128
    send_place = target * capacity + slot_pos
    outgoing = jnp.zeros((tile_total * capacity, width), jnp.bfloat16).at[send_place].set(rows_out)
    got = lax.all_to_all(
        outgoing.reshape(tile_total, capacity, width),
        ("mx", "my"),
        split_axis=0,
        concat_axis=0,
        tiled=True,
    ).reshape(-1, width)
    mark_row = got[:, feature].astype(jnp.int32)
    mark_col = got[:, feature + 1].astype(jnp.int32)
    unit_ids = jnp.where(got[:, feature + 2] > 0.5, mark_row * cols_tile + mark_col, -1)
    numerator, counter = accumulate(
        unit_ids, got, lambda m: m, rows_tile * cols_tile // 512, feature
    )
    numerator = numerator.reshape(rows_tile, cols_tile, feature)
    counter = counter[:, 2].reshape(rows_tile, cols_tile)

    g_rows = jnp.asarray(band_matrix(rows_tile))
    g_cols = jnp.asarray(band_matrix(cols_tile))
    last = cols_tile - RADIUS
    lead = numerator[:, :RADIUS].astype(jnp.bfloat16)
    from_left, from_right = exchange(lead, numerator[:, last:].astype(jnp.bfloat16), "my")
    from_left, from_right = from_left.astype(jnp.float32), from_right.astype(jnp.float32)
    hits_left, hits_right = exchange(counter[:, :RADIUS], counter[:, last:], "my")
    ext_num = jnp.concatenate([from_left, numerator, from_right], axis=1)
    ext_hits = jnp.concatenate([hits_left, counter, hits_right], axis=1)
    col_num = jnp.einsum("ck,rke->rce", g_cols, ext_num, precision=HI)
    col_hits = jnp.einsum("ck,rk->rc", g_cols, ext_hits, precision=HI)
    last = rows_tile - RADIUS
    above, below = exchange(col_num[:RADIUS], col_num[last:], "mx")
    hits_above, hits_below = exchange(col_hits[:RADIUS], col_hits[last:], "mx")
    inner_hits = jnp.einsum("rk,kc->rc", g_rows[RADIUS:last, RADIUS : RADIUS + rows_tile], col_hits, precision=HI)
    inv_inner = 1.0 / (inner_hits + 8.0)
    inv = jnp.concatenate([jnp.zeros_like(inv_inner[:RADIUS]), inv_inner, jnp.zeros_like(inv_inner[:RADIUS])])
    inv = inv[:, :, None]
    edge_top = jnp.concatenate([hits_above, col_hits[: 2 * RADIUS]], axis=0)
    edge_bottom = jnp.concatenate([col_hits[last - RADIUS :], hits_below], axis=0)
    g_edge = g_rows[:RADIUS, : 3 * RADIUS]
    top_hits = jnp.einsum("rk,kc->rc", g_edge, edge_top, precision=HI)
    bottom_hits = jnp.einsum("rk,kc->rc", g_edge, edge_bottom, precision=HI)
    inv_edges = (1.0 / (jnp.concatenate([top_hits, bottom_hits], axis=0) + 8.0))[:, :, None]
    partial = finish_inner(col_num, codebook, inv)
    return finish_edges(above, col_num, below, codebook, inv_edges, partial)


def solution(mesh):
    return jax.shard_map(
        on_device,
        mesh=mesh,
        in_specs=(
            P(("mx", "my"), None),
            P(("mx", "my"), None),
            P(("mx", "my")),
            P("mx", "my", None),
        ),
        out_specs=P("mx", "my", None),
        check_vma=False,
    )
```

```python
import math

import jax
import jax.numpy as jnp
import numpy as np
from jax import lax
from jax.experimental import pallas as pl
from jax.experimental.pallas import tpu as pltpu
from jax.sharding import PartitionSpec as P

RADIUS = 8
HI = lax.Precision.HIGH


def band_matrix(out_len):
    ext = out_len + 2 * RADIUS
    mat = np.zeros((out_len, ext), np.float32)
    for r in range(out_len):
        for k in range(-RADIUS, RADIUS + 1):
            mat[r, r + k + RADIUS] = math.exp(-2.0 * k * k / RADIUS**2)
    return mat


def accumulate(ids, docs, rows_tile, cols_tile, feature, col_blocks, prior=None):
    rows, width = docs.shape
    band = rows_tile * RADIUS
    picks = jnp.asarray(col_blocks, jnp.int32)

    def kernel(picks_ref, ids_ref, docs_ref, *refs):
        num_ref, hits_ref = refs[-2:]
        place = lax.broadcasted_iota(jnp.int32, (band, rows), 0)
        first_col = picks_ref[pl.program_id(0)] * RADIUS
        units = (place // RADIUS) * cols_tile + first_col + place % RADIUS
        one_hot = (units == ids_ref[...]).astype(jnp.bfloat16)
        sums = jnp.dot(one_hot, docs_ref[...], preferred_element_type=jnp.float32)
        num_ref[...] = sums[:, :feature].reshape(rows_tile, RADIUS, feature)
        hits_ref[...] = sums[:, feature:].reshape(rows_tile, RADIUS, width - feature)

    out_specs = [
        pl.BlockSpec((rows_tile, RADIUS, feature), lambda j, p: (0, p[j], 0)),
        pl.BlockSpec((rows_tile, RADIUS, width - feature), lambda j, p: (0, p[j], 0)),
    ]
    in_specs = [
        pl.BlockSpec((1, rows), lambda j, p: (0, 0)),
        pl.BlockSpec((rows, width), lambda j, p: (0, 0)),
    ]
    operands = [ids.reshape(1, rows), docs]
    aliases = {}
    if prior is not None:
        in_specs += [pl.BlockSpec(memory_space=pl.ANY)] * 2
        operands += list(prior)
        aliases = {3: 0, 4: 1}
    return pl.pallas_call(
        kernel,
        grid_spec=pltpu.PrefetchScalarGridSpec(
            num_scalar_prefetch=1,
            grid=(len(col_blocks),),
            in_specs=in_specs,
            out_specs=out_specs,
        ),
        out_shape=[
            jax.ShapeDtypeStruct((rows_tile, cols_tile, feature), jnp.float32),
            jax.ShapeDtypeStruct((rows_tile, cols_tile, width - feature), jnp.float32),
        ],
        input_output_aliases=aliases,
    )(picks, *operands)


def finish_inner(middle, codebook, inv):
    rows, cols, feature = middle.shape
    lanes = 128

    def kernel(mid_ref, cb_ref, inv_ref, out_ref):
        ext = mid_ref
        taps = [math.exp(-2.0 * k * k / RADIUS**2) for k in range(RADIUS + 1)]

        def body(r, carry):
            acc = taps[0] * ext[r]
            for k in range(1, RADIUS + 1):
                acc = acc + taps[k] * (ext[r - k] + ext[r + k])
            upd = (acc + 8.0 * cb_ref[r].astype(jnp.float32)) * inv_ref[r]
            out_ref[r] = upd.astype(out_ref.dtype)
            return carry

        lax.fori_loop(RADIUS, rows - RADIUS, body, 0, unroll=2)

    slab_spec = pl.BlockSpec((rows, cols, lanes), lambda j: (0, 0, j))
    return pl.pallas_call(
        kernel,
        grid=(feature // lanes,),
        in_specs=[slab_spec, slab_spec, pl.BlockSpec((rows, cols, 1), lambda j: (0, 0, 0))],
        out_specs=slab_spec,
        out_shape=jax.ShapeDtypeStruct(codebook.shape, codebook.dtype),
    )(middle, codebook, inv)


def finish_edges(above, middle, below, codebook, inv, partial):
    rows, cols, feature = middle.shape
    lanes = 128
    near = 2 * RADIUS
    last_edge = rows // RADIUS - 1
    taps = [math.exp(-2.0 * k * k / RADIUS**2) for k in range(RADIUS + 1)]

    def kernel(above_ref, mid_ref, below_ref, cb_ref, inv_ref, prev_ref, out_ref, ext_ref):
        del prev_ref
        side = pl.program_id(0)

        @pl.when(side == 0)
        def _():
            ext_ref[0:RADIUS] = above_ref[...]
            ext_ref[RADIUS:] = mid_ref[...]

        @pl.when(side == 1)
        def _():
            ext_ref[0:near] = mid_ref[...]
            ext_ref[near:] = below_ref[...]

        def body(r, carry):
            centre = r + RADIUS
            scale = inv_ref[r]
            for lane in range(0, feature, lanes):
                part = pl.ds(lane, lanes)
                acc = taps[0] * ext_ref[centre, :, part]
                for k in range(1, RADIUS + 1):
                    acc = acc + taps[k] * (ext_ref[centre - k, :, part] + ext_ref[centre + k, :, part])
                upd = (acc + 8.0 * cb_ref[r, :, part].astype(jnp.float32)) * scale
                out_ref[r, :, part] = upd.astype(out_ref.dtype)
            return carry

        lax.fori_loop(0, RADIUS, body, 0)

    halo_spec = pl.BlockSpec((RADIUS, cols, feature), lambda i: (0, 0, 0))
    edge_spec = pl.BlockSpec((RADIUS, cols, feature), lambda i: (i * last_edge, 0, 0))
    return pl.pallas_call(
        kernel,
        grid=(2,),
        in_specs=[
            halo_spec,
            pl.BlockSpec((near, cols, feature), lambda i: (i * (rows // near - 1), 0, 0)),
            halo_spec,
            edge_spec,
            pl.BlockSpec((RADIUS, cols, 1), lambda i: (i, 0, 0)),
            pl.BlockSpec(memory_space=pl.ANY),
        ],
        out_specs=edge_spec,
        out_shape=jax.ShapeDtypeStruct(codebook.shape, codebook.dtype),
        scratch_shapes=[pltpu.VMEM((near + RADIUS, cols, feature), jnp.float32)],
        input_output_aliases={5: 0},
    )(above, middle, below, codebook, inv, partial)


def exchange(lead, last, axis):
    devices = lax.axis_size(axis)
    up = [(i, i + 1) for i in range(devices - 1)]
    down = [(j, i) for i, j in up]
    return lax.ppermute(last, axis, up), lax.ppermute(lead, axis, down)


def on_device(documents, owner_tile, unit_in_tile, codebook):
    rows_mx = lax.axis_size("mx")
    cols_my = lax.axis_size("my")
    tile_total = rows_mx * cols_my
    rows_tile, cols_tile, feature = codebook.shape
    doc_count = documents.shape[0]
    capacity = max(2, 2 * doc_count // tile_total)
    target = owner_tile[:, 0]
    tile_hits = (target[:, None] == jnp.arange(tile_total, dtype=jnp.int32)[None, :]).astype(
        jnp.int32
    )
    earlier = jnp.cumsum(tile_hits, axis=0) - tile_hits
    slot_pos = jnp.sum(earlier * tile_hits, axis=1)
    unit_row = unit_in_tile // cols_tile
    unit_col = unit_in_tile % cols_tile
    extra = jnp.zeros((doc_count, 128), jnp.bfloat16)
    extra = extra.at[:, 0].set(unit_row.astype(jnp.bfloat16))
    extra = extra.at[:, 1].set(unit_col.astype(jnp.bfloat16))
    extra = extra.at[:, 2].set(1.0)
    rows_out = jnp.concatenate([documents, extra], axis=1)
    width = feature + 128
    send_place = target * capacity + slot_pos
    outgoing = jnp.zeros((tile_total * capacity, width), jnp.bfloat16).at[send_place].set(rows_out)
    got = lax.all_to_all(
        outgoing.reshape(tile_total, capacity, width),
        ("mx", "my"),
        split_axis=0,
        concat_axis=0,
        tiled=True,
    ).reshape(-1, width)
    mark_row = got[:, feature].astype(jnp.int32)
    mark_col = got[:, feature + 1].astype(jnp.int32)
    unit_ids = jnp.where(got[:, feature + 2] > 0.5, mark_row * cols_tile + mark_col, -1)
    col_total = cols_tile // RADIUS
    bands = accumulate(unit_ids, got, rows_tile, cols_tile, feature, [0, col_total - 1])
    last = cols_tile - RADIUS
    lead, tail = bands[0][:, :RADIUS], bands[0][:, last:]
    hits_lead, hits_tail = bands[1][:, :RADIUS, 2], bands[1][:, last:, 2]
    from_left, from_right = exchange(lead, tail, "my")
    hits_left, hits_right = exchange(hits_lead, hits_tail, "my")
    inner = list(range(1, col_total - 1))
    numerator, counter = accumulate(unit_ids, got, rows_tile, cols_tile, feature, inner, bands)
    counter = counter[:, :, 2]

    g_rows = jnp.asarray(band_matrix(rows_tile))
    g_cols = jnp.asarray(band_matrix(cols_tile))
    ext_num = jnp.concatenate([from_left, numerator, from_right], axis=1)
    ext_hits = jnp.concatenate([hits_left, counter, hits_right], axis=1)
    col_num = jnp.einsum("ck,rke->rce", g_cols, ext_num, precision=HI)
    col_hits = jnp.einsum("ck,rk->rc", g_cols, ext_hits, precision=HI)
    last = rows_tile - RADIUS
    above, below = exchange(col_num[:RADIUS], col_num[last:], "mx")
    hits_above, hits_below = exchange(col_hits[:RADIUS], col_hits[last:], "mx")
    inner_hits = jnp.einsum("rk,kc->rc", g_rows[RADIUS:last, RADIUS : RADIUS + rows_tile], col_hits, precision=HI)
    inv_inner = 1.0 / (inner_hits + 8.0)
    inv = jnp.concatenate([jnp.zeros_like(inv_inner[:RADIUS]), inv_inner, jnp.zeros_like(inv_inner[:RADIUS])])
    inv = inv[:, :, None]
    edge_top = jnp.concatenate([hits_above, col_hits[: 2 * RADIUS]], axis=0)
    edge_bottom = jnp.concatenate([col_hits[last - RADIUS :], hits_below], axis=0)
    g_edge = g_rows[:RADIUS, : 3 * RADIUS]
    top_hits = jnp.einsum("rk,kc->rc", g_edge, edge_top, precision=HI)
    bottom_hits = jnp.einsum("rk,kc->rc", g_edge, edge_bottom, precision=HI)
    inv_edges = (1.0 / (jnp.concatenate([top_hits, bottom_hits], axis=0) + 8.0))[:, :, None]
    partial = finish_inner(col_num, codebook, inv)
    return finish_edges(above, col_num, below, codebook, inv_edges, partial)


def solution(mesh):
    return jax.shard_map(
        on_device,
        mesh=mesh,
        in_specs=(
            P(("mx", "my"), None),
            P(("mx", "my"), None),
            P(("mx", "my")),
            P("mx", "my", None),
        ),
        out_specs=P("mx", "my", None),
        check_vma=False,
    )
```

```python
import math

import jax
import jax.numpy as jnp
import numpy as np
from jax import lax
from jax.experimental import pallas as pl
from jax.experimental.pallas import tpu as pltpu
from jax.sharding import PartitionSpec as P

RADIUS = 8
HI = lax.Precision.HIGH


def band_matrix(out_len):
    ext = out_len + 2 * RADIUS
    mat = np.zeros((out_len, ext), np.float32)
    for r in range(out_len):
        for k in range(-RADIUS, RADIUS + 1):
            mat[r, r + k + RADIUS] = math.exp(-2.0 * k * k / RADIUS**2)
    return mat


def accumulate(ids, docs, rows_tile, cols_tile, feature, col_blocks, prior=None):
    rows, width = docs.shape
    band = rows_tile * RADIUS
    picks = jnp.asarray(col_blocks, jnp.int32)

    def kernel(picks_ref, ids_ref, docs_ref, *refs):
        num_ref, hits_ref = refs[-2:]
        place = lax.broadcasted_iota(jnp.int32, (band, rows), 0)
        first_col = picks_ref[pl.program_id(0)] * RADIUS
        units = (place // RADIUS) * cols_tile + first_col + place % RADIUS
        one_hot = (units == ids_ref[...]).astype(jnp.bfloat16)
        sums = jnp.dot(one_hot, docs_ref[...], preferred_element_type=jnp.float32)
        num_ref[...] = sums[:, :feature].reshape(rows_tile, RADIUS, feature)
        hits_ref[...] = sums[:, feature:].reshape(rows_tile, RADIUS, width - feature)

    out_specs = [
        pl.BlockSpec((rows_tile, RADIUS, feature), lambda j, p: (0, p[j], 0)),
        pl.BlockSpec((rows_tile, RADIUS, width - feature), lambda j, p: (0, p[j], 0)),
    ]
    in_specs = [
        pl.BlockSpec((1, rows), lambda j, p: (0, 0)),
        pl.BlockSpec((rows, width), lambda j, p: (0, 0)),
    ]
    operands = [ids.reshape(1, rows), docs]
    aliases = {}
    if prior is not None:
        in_specs += [pl.BlockSpec(memory_space=pl.ANY)] * 2
        operands += list(prior)
        aliases = {3: 0, 4: 1}
    return pl.pallas_call(
        kernel,
        grid_spec=pltpu.PrefetchScalarGridSpec(
            num_scalar_prefetch=1,
            grid=(len(col_blocks),),
            in_specs=in_specs,
            out_specs=out_specs,
        ),
        out_shape=[
            jax.ShapeDtypeStruct((rows_tile, cols_tile, feature), jnp.float32),
            jax.ShapeDtypeStruct((rows_tile, cols_tile, width - feature), jnp.float32),
        ],
        input_output_aliases=aliases,
    )(picks, *operands)


def finish_inner(middle, codebook, inv):
    rows, cols, feature = middle.shape
    lanes = 128

    def kernel(mid_ref, cb_ref, inv_ref, out_ref):
        ext = mid_ref
        taps = [math.exp(-2.0 * k * k / RADIUS**2) for k in range(RADIUS + 1)]

        def body(r, carry):
            acc = taps[0] * ext[r]
            for k in range(1, RADIUS + 1):
                acc = acc + taps[k] * (ext[r - k] + ext[r + k])
            upd = (acc + 8.0 * cb_ref[r].astype(jnp.float32)) * inv_ref[r]
            out_ref[r] = upd.astype(out_ref.dtype)
            return carry

        lax.fori_loop(RADIUS, rows - RADIUS, body, 0, unroll=2)

    slab_spec = pl.BlockSpec((rows, cols, lanes), lambda j: (0, 0, j))
    return pl.pallas_call(
        kernel,
        grid=(feature // lanes,),
        in_specs=[slab_spec, slab_spec, pl.BlockSpec((rows, cols, 1), lambda j: (0, 0, 0))],
        out_specs=slab_spec,
        out_shape=jax.ShapeDtypeStruct(codebook.shape, codebook.dtype),
    )(middle, codebook, inv)


def finish_edges(above, middle, below, codebook, inv, partial):
    rows, cols, feature = middle.shape
    lanes = 128
    near = 2 * RADIUS
    last_edge = rows // RADIUS - 1
    taps = [math.exp(-2.0 * k * k / RADIUS**2) for k in range(RADIUS + 1)]

    def kernel(above_ref, mid_ref, below_ref, cb_ref, inv_ref, prev_ref, out_ref, ext_ref):
        del prev_ref
        side = pl.program_id(0)

        @pl.when(side == 0)
        def _():
            ext_ref[0:RADIUS] = above_ref[...]
            ext_ref[RADIUS:] = mid_ref[...]

        @pl.when(side == 1)
        def _():
            ext_ref[0:near] = mid_ref[...]
            ext_ref[near:] = below_ref[...]

        def body(r, carry):
            centre = r + RADIUS
            scale = inv_ref[r]
            for lane in range(0, feature, lanes):
                part = pl.ds(lane, lanes)
                acc = taps[0] * ext_ref[centre, :, part]
                for k in range(1, RADIUS + 1):
                    acc = acc + taps[k] * (ext_ref[centre - k, :, part] + ext_ref[centre + k, :, part])
                upd = (acc + 8.0 * cb_ref[r, :, part].astype(jnp.float32)) * scale
                out_ref[r, :, part] = upd.astype(out_ref.dtype)
            return carry

        lax.fori_loop(0, RADIUS, body, 0)

    halo_spec = pl.BlockSpec((RADIUS, cols, feature), lambda i: (0, 0, 0))
    edge_spec = pl.BlockSpec((RADIUS, cols, feature), lambda i: (i * last_edge, 0, 0))
    return pl.pallas_call(
        kernel,
        grid=(2,),
        in_specs=[
            halo_spec,
            pl.BlockSpec((near, cols, feature), lambda i: (i * (rows // near - 1), 0, 0)),
            halo_spec,
            edge_spec,
            pl.BlockSpec((RADIUS, cols, 1), lambda i: (i, 0, 0)),
            pl.BlockSpec(memory_space=pl.ANY),
        ],
        out_specs=edge_spec,
        out_shape=jax.ShapeDtypeStruct(codebook.shape, codebook.dtype),
        scratch_shapes=[pltpu.VMEM((near + RADIUS, cols, feature), jnp.float32)],
        input_output_aliases={5: 0},
    )(above, middle, below, codebook, inv, partial)


def exchange(lead, last, axis):
    devices = lax.axis_size(axis)
    up = [(i, i + 1) for i in range(devices - 1)]
    down = [(j, i) for i, j in up]
    return lax.ppermute(last, axis, up), lax.ppermute(lead, axis, down)


def on_device(documents, owner_tile, unit_in_tile, codebook):
    rows_mx = lax.axis_size("mx")
    cols_my = lax.axis_size("my")
    tile_total = rows_mx * cols_my
    rows_tile, cols_tile, feature = codebook.shape
    doc_count = documents.shape[0]
    capacity = max(2, 2 * doc_count // tile_total)
    target = owner_tile[:, 0]
    tile_hits = (target[:, None] == jnp.arange(tile_total, dtype=jnp.int32)[None, :]).astype(
        jnp.int32
    )
    earlier = jnp.cumsum(tile_hits, axis=0) - tile_hits
    slot_pos = jnp.sum(earlier * tile_hits, axis=1)
    unit_row = unit_in_tile // cols_tile
    unit_col = unit_in_tile % cols_tile
    extra = jnp.zeros((doc_count, 128), jnp.bfloat16)
    extra = extra.at[:, 0].set(unit_row.astype(jnp.bfloat16))
    extra = extra.at[:, 1].set(unit_col.astype(jnp.bfloat16))
    extra = extra.at[:, 2].set(1.0)
    rows_out = jnp.concatenate([documents, extra], axis=1)
    width = feature + 128
    send_place = target * capacity + slot_pos
    outgoing = jnp.zeros((tile_total * capacity, width), jnp.bfloat16).at[send_place].set(rows_out)
    got = lax.all_to_all(
        outgoing.reshape(tile_total, capacity, width),
        ("mx", "my"),
        split_axis=0,
        concat_axis=0,
        tiled=True,
    ).reshape(-1, width)
    mark_row = got[:, feature].astype(jnp.int32)
    mark_col = got[:, feature + 1].astype(jnp.int32)
    unit_ids = jnp.where(got[:, feature + 2] > 0.5, mark_row * cols_tile + mark_col, -1)
    col_total = cols_tile // RADIUS
    bands = accumulate(unit_ids, got, rows_tile, cols_tile, feature, [0, col_total - 1])
    last = cols_tile - RADIUS
    lead = jnp.concatenate([bands[0][:, :RADIUS], bands[1][:, :RADIUS]], axis=2)
    tail = jnp.concatenate([bands[0][:, last:], bands[1][:, last:]], axis=2)
    from_left, from_right = exchange(lead, tail, "my")
    hits_left, hits_right = from_left[:, :, feature + 2], from_right[:, :, feature + 2]
    from_left, from_right = from_left[:, :, :feature], from_right[:, :, :feature]
    inner = list(range(1, col_total - 1))
    numerator, counter = accumulate(unit_ids, got, rows_tile, cols_tile, feature, inner, bands)
    counter = counter[:, :, 2]

    g_rows = jnp.asarray(band_matrix(rows_tile))
    g_cols = jnp.asarray(band_matrix(cols_tile))
    ext_num = jnp.concatenate([from_left, numerator, from_right], axis=1)
    ext_hits = jnp.concatenate([hits_left, counter, hits_right], axis=1)
    col_num = jnp.einsum("ck,rke->rce", g_cols, ext_num, precision=HI)
    col_hits = jnp.einsum("ck,rk->rc", g_cols, ext_hits, precision=HI)
    last = rows_tile - RADIUS
    def with_hits(rows):
        hit_lanes = jnp.pad(col_hits[rows][:, :, None], ((0, 0), (0, 0), (0, 127)))
        return jnp.concatenate([col_num[rows], hit_lanes], axis=2)

    above, below = exchange(with_hits(slice(0, RADIUS)), with_hits(slice(last, rows_tile)), "mx")
    hits_above, hits_below = above[:, :, feature], below[:, :, feature]
    inner_hits = jnp.einsum("rk,kc->rc", g_rows[RADIUS:last, RADIUS : RADIUS + rows_tile], col_hits, precision=HI)
    inv_inner = 1.0 / (inner_hits + 8.0)
    inv = jnp.concatenate([jnp.zeros_like(inv_inner[:RADIUS]), inv_inner, jnp.zeros_like(inv_inner[:RADIUS])])
    inv = inv[:, :, None]
    edge_top = jnp.concatenate([hits_above, col_hits[: 2 * RADIUS]], axis=0)
    edge_bottom = jnp.concatenate([col_hits[last - RADIUS :], hits_below], axis=0)
    g_edge = g_rows[:RADIUS, : 3 * RADIUS]
    top_hits = jnp.einsum("rk,kc->rc", g_edge, edge_top, precision=HI)
    bottom_hits = jnp.einsum("rk,kc->rc", g_edge, edge_bottom, precision=HI)
    inv_edges = (1.0 / (jnp.concatenate([top_hits, bottom_hits], axis=0) + 8.0))[:, :, None]
    partial = finish_inner(col_num, codebook, inv)
    return finish_edges(above, col_num, below, codebook, inv_edges, partial)


def solution(mesh):
    return jax.shard_map(
        on_device,
        mesh=mesh,
        in_specs=(
            P(("mx", "my"), None),
            P(("mx", "my"), None),
            P(("mx", "my")),
            P("mx", "my", None),
        ),
        out_specs=P("mx", "my", None),
        check_vma=False,
    )
```

```python
import math

import jax
import jax.numpy as jnp
import numpy as np
from jax import lax
from jax.experimental import pallas as pl
from jax.experimental.pallas import tpu as pltpu
from jax.sharding import PartitionSpec as P

RADIUS = 8
HI = lax.Precision.HIGH


def band_matrix(out_len):
    ext = out_len + 2 * RADIUS
    mat = np.zeros((out_len, ext), np.float32)
    for r in range(out_len):
        for k in range(-RADIUS, RADIUS + 1):
            mat[r, r + k + RADIUS] = math.exp(-2.0 * k * k / RADIUS**2)
    return mat


def accumulate(ids, docs, rows_tile, cols_tile, feature, col_blocks, prior=None):
    rows, width = docs.shape
    band = rows_tile * RADIUS
    picks = jnp.asarray(col_blocks, jnp.int32)

    def kernel(picks_ref, ids_ref, docs_ref, *refs):
        num_ref, hits_ref = refs[-2:]
        place = lax.broadcasted_iota(jnp.int32, (band, rows), 0)
        first_col = picks_ref[pl.program_id(0)] * RADIUS
        units = (place // RADIUS) * cols_tile + first_col + place % RADIUS
        one_hot = (units == ids_ref[...]).astype(jnp.bfloat16)
        sums = jnp.dot(one_hot, docs_ref[...], preferred_element_type=jnp.float32)
        num_ref[...] = sums[:, :feature].reshape(rows_tile, RADIUS, feature)
        hits_ref[...] = sums[:, feature:].reshape(rows_tile, RADIUS, width - feature)

    out_specs = [
        pl.BlockSpec((rows_tile, RADIUS, feature), lambda j, p: (0, p[j], 0)),
        pl.BlockSpec((rows_tile, RADIUS, width - feature), lambda j, p: (0, p[j], 0)),
    ]
    in_specs = [
        pl.BlockSpec((1, rows), lambda j, p: (0, 0)),
        pl.BlockSpec((rows, width), lambda j, p: (0, 0)),
    ]
    operands = [ids.reshape(1, rows), docs]
    aliases = {}
    if prior is not None:
        in_specs += [pl.BlockSpec(memory_space=pl.ANY)] * 2
        operands += list(prior)
        aliases = {3: 0, 4: 1}
    return pl.pallas_call(
        kernel,
        grid_spec=pltpu.PrefetchScalarGridSpec(
            num_scalar_prefetch=1,
            grid=(len(col_blocks),),
            in_specs=in_specs,
            out_specs=out_specs,
        ),
        out_shape=[
            jax.ShapeDtypeStruct((rows_tile, cols_tile, feature), jnp.float32),
            jax.ShapeDtypeStruct((rows_tile, cols_tile, width - feature), jnp.float32),
        ],
        input_output_aliases=aliases,
    )(picks, *operands)


TAPS = [math.exp(-2.0 * k * k / RADIUS**2) for k in range(RADIUS + 1)]
GROUP = 4


def row_group(read, cb_ref, inv_ref, out_ref, first, cols, lanes):
    for c0 in range(0, cols, 8):
        window = [read(j, c0, lanes) for j in range(GROUP + 2 * RADIUS)]
        for q in range(GROUP):
            centre = q + RADIUS
            acc = TAPS[0] * window[centre]
            for k in range(1, RADIUS + 1):
                acc = acc + TAPS[k] * (window[centre - k] + window[centre + k])
            r = first + q
            base = cb_ref[r, pl.ds(c0, 8), lanes].astype(jnp.float32)
            upd = (acc + 8.0 * base) * inv_ref[r, pl.ds(c0, 8), :]
            out_ref[r, pl.ds(c0, 8), lanes] = upd.astype(out_ref.dtype)


def finish_inner(middle, codebook, inv):
    rows, cols, feature = middle.shape
    lanes = 128

    def kernel(mid_ref, cb_ref, inv_ref, out_ref):
        def body(i, carry):
            first = RADIUS + i * GROUP

            def read(j, c0, part):
                return mid_ref[first + j - RADIUS, pl.ds(c0, 8), part]

            row_group(read, cb_ref, inv_ref, out_ref, first, cols, slice(None))
            return carry

        lax.fori_loop(0, (rows - 2 * RADIUS) // GROUP, body, 0)

    slab_spec = pl.BlockSpec((rows, cols, lanes), lambda j: (0, 0, j))
    return pl.pallas_call(
        kernel,
        grid=(feature // lanes,),
        in_specs=[slab_spec, slab_spec, pl.BlockSpec((rows, cols, 1), lambda j: (0, 0, 0))],
        out_specs=slab_spec,
        out_shape=jax.ShapeDtypeStruct(codebook.shape, codebook.dtype),
    )(middle, codebook, inv)


def finish_edges(above, middle, below, codebook, inv, partial):
    rows, cols, feature = middle.shape
    lanes = 128
    near = 2 * RADIUS
    last_edge = rows // RADIUS - 1

    def kernel(above_ref, mid_ref, below_ref, cb_ref, inv_ref, prev_ref, out_ref, ext_ref):
        del prev_ref
        side = pl.program_id(0)

        @pl.when(side == 0)
        def _():
            ext_ref[0:RADIUS] = above_ref[...]
            ext_ref[RADIUS:] = mid_ref[...]

        @pl.when(side == 1)
        def _():
            ext_ref[0:near] = mid_ref[...]
            ext_ref[near:] = below_ref[...]

        def body(i, carry):
            first = i * GROUP

            def read(j, c0, part):
                return ext_ref[first + j, pl.ds(c0, 8), part]

            for lane in range(0, feature, lanes):
                row_group(read, cb_ref, inv_ref, out_ref, first, cols, pl.ds(lane, lanes))
            return carry

        lax.fori_loop(0, RADIUS // GROUP, body, 0)

    halo_spec = pl.BlockSpec((RADIUS, cols, feature), lambda i: (0, 0, 0))
    edge_spec = pl.BlockSpec((RADIUS, cols, feature), lambda i: (i * last_edge, 0, 0))
    return pl.pallas_call(
        kernel,
        grid=(2,),
        in_specs=[
            halo_spec,
            pl.BlockSpec((near, cols, feature), lambda i: (i * (rows // near - 1), 0, 0)),
            halo_spec,
            edge_spec,
            pl.BlockSpec((RADIUS, cols, 1), lambda i: (i, 0, 0)),
            pl.BlockSpec(memory_space=pl.ANY),
        ],
        out_specs=edge_spec,
        out_shape=jax.ShapeDtypeStruct(codebook.shape, codebook.dtype),
        scratch_shapes=[pltpu.VMEM((near + RADIUS, cols, feature), jnp.float32)],
        input_output_aliases={5: 0},
    )(above, middle, below, codebook, inv, partial)


def exchange(lead, last, axis):
    devices = lax.axis_size(axis)
    up = [(i, i + 1) for i in range(devices - 1)]
    down = [(j, i) for i, j in up]
    return lax.ppermute(last, axis, up), lax.ppermute(lead, axis, down)


def on_device(documents, owner_tile, unit_in_tile, codebook):
    rows_mx = lax.axis_size("mx")
    cols_my = lax.axis_size("my")
    tile_total = rows_mx * cols_my
    rows_tile, cols_tile, feature = codebook.shape
    doc_count = documents.shape[0]
    capacity = max(2, 2 * doc_count // tile_total)
    target = owner_tile[:, 0]
    tile_hits = (target[:, None] == jnp.arange(tile_total, dtype=jnp.int32)[None, :]).astype(
        jnp.int32
    )
    earlier = jnp.cumsum(tile_hits, axis=0) - tile_hits
    slot_pos = jnp.sum(earlier * tile_hits, axis=1)
    unit_row = unit_in_tile // cols_tile
    unit_col = unit_in_tile % cols_tile
    extra = jnp.zeros((doc_count, 128), jnp.bfloat16)
    extra = extra.at[:, 0].set(unit_row.astype(jnp.bfloat16))
    extra = extra.at[:, 1].set(unit_col.astype(jnp.bfloat16))
    extra = extra.at[:, 2].set(1.0)
    rows_out = jnp.concatenate([documents, extra], axis=1)
    width = feature + 128
    send_place = target * capacity + slot_pos
    outgoing = jnp.zeros((tile_total * capacity, width), jnp.bfloat16).at[send_place].set(rows_out)
    got = lax.all_to_all(
        outgoing.reshape(tile_total, capacity, width),
        ("mx", "my"),
        split_axis=0,
        concat_axis=0,
        tiled=True,
    ).reshape(-1, width)
    mark_row = got[:, feature].astype(jnp.int32)
    mark_col = got[:, feature + 1].astype(jnp.int32)
    unit_ids = jnp.where(got[:, feature + 2] > 0.5, mark_row * cols_tile + mark_col, -1)
    col_total = cols_tile // RADIUS
    bands = accumulate(unit_ids, got, rows_tile, cols_tile, feature, [0, col_total - 1])
    last = cols_tile - RADIUS
    lead = jnp.concatenate([bands[0][:, :RADIUS], bands[1][:, :RADIUS]], axis=2)
    tail = jnp.concatenate([bands[0][:, last:], bands[1][:, last:]], axis=2)
    from_left, from_right = exchange(lead, tail, "my")
    hits_left, hits_right = from_left[:, :, feature + 2], from_right[:, :, feature + 2]
    from_left, from_right = from_left[:, :, :feature], from_right[:, :, :feature]
    inner = list(range(1, col_total - 1))
    numerator, counter = accumulate(unit_ids, got, rows_tile, cols_tile, feature, inner, bands)
    counter = counter[:, :, 2]

    g_rows = jnp.asarray(band_matrix(rows_tile))
    g_cols = jnp.asarray(band_matrix(cols_tile))
    ext_num = jnp.concatenate([from_left, numerator, from_right], axis=1)
    ext_hits = jnp.concatenate([hits_left, counter, hits_right], axis=1)
    col_num = jnp.einsum("ck,rke->rce", g_cols, ext_num, precision=HI)
    col_hits = jnp.einsum("ck,rk->rc", g_cols, ext_hits, precision=HI)
    last = rows_tile - RADIUS
    def with_hits(rows):
        hit_lanes = jnp.pad(col_hits[rows][:, :, None], ((0, 0), (0, 0), (0, 127)))
        return jnp.concatenate([col_num[rows], hit_lanes], axis=2)

    above, below = exchange(with_hits(slice(0, RADIUS)), with_hits(slice(last, rows_tile)), "mx")
    hits_above, hits_below = above[:, :, feature], below[:, :, feature]
    inner_hits = jnp.einsum("rk,kc->rc", g_rows[RADIUS:last, RADIUS : RADIUS + rows_tile], col_hits, precision=HI)
    inv_inner = 1.0 / (inner_hits + 8.0)
    inv = jnp.concatenate([jnp.zeros_like(inv_inner[:RADIUS]), inv_inner, jnp.zeros_like(inv_inner[:RADIUS])])
    inv = inv[:, :, None]
    edge_top = jnp.concatenate([hits_above, col_hits[: 2 * RADIUS]], axis=0)
    edge_bottom = jnp.concatenate([col_hits[last - RADIUS :], hits_below], axis=0)
    g_edge = g_rows[:RADIUS, : 3 * RADIUS]
    top_hits = jnp.einsum("rk,kc->rc", g_edge, edge_top, precision=HI)
    bottom_hits = jnp.einsum("rk,kc->rc", g_edge, edge_bottom, precision=HI)
    inv_edges = (1.0 / (jnp.concatenate([top_hits, bottom_hits], axis=0) + 8.0))[:, :, None]
    partial = finish_inner(col_num, codebook, inv)
    return finish_edges(above, col_num, below, codebook, inv_edges, partial)


def solution(mesh):
    return jax.shard_map(
        on_device,
        mesh=mesh,
        in_specs=(
            P(("mx", "my"), None),
            P(("mx", "my"), None),
            P(("mx", "my")),
            P("mx", "my", None),
        ),
        out_specs=P("mx", "my", None),
        check_vma=False,
    )
```

```python
import math

import jax
import jax.numpy as jnp
import numpy as np
from jax import lax
from jax.experimental import pallas as pl
from jax.experimental.pallas import tpu as pltpu
from jax.sharding import PartitionSpec as P

RADIUS = 8
HI = lax.Precision.HIGH


def band_matrix(out_len):
    ext = out_len + 2 * RADIUS
    mat = np.zeros((out_len, ext), np.float32)
    for r in range(out_len):
        for k in range(-RADIUS, RADIUS + 1):
            mat[r, r + k + RADIUS] = math.exp(-2.0 * k * k / RADIUS**2)
    return mat


def accumulate(ids, docs, rows_tile, cols_tile, feature, col_blocks, prior=None):
    rows, width = docs.shape
    band = rows_tile * RADIUS
    picks = jnp.asarray(col_blocks, jnp.int32)

    def kernel(picks_ref, ids_ref, docs_ref, *refs):
        num_ref, hits_ref = refs[-2:]
        place = lax.broadcasted_iota(jnp.int32, (band, rows), 0)
        first_col = picks_ref[pl.program_id(0)] * RADIUS
        units = (place // RADIUS) * cols_tile + first_col + place % RADIUS
        one_hot = (units == ids_ref[...]).astype(jnp.bfloat16)
        sums = jnp.dot(one_hot, docs_ref[...], preferred_element_type=jnp.float32)
        num_ref[...] = sums[:, :feature].reshape(rows_tile, RADIUS, feature)
        hits_ref[...] = sums[:, feature:].reshape(rows_tile, RADIUS, width - feature)

    out_specs = [
        pl.BlockSpec((rows_tile, RADIUS, feature), lambda j, p: (0, p[j], 0)),
        pl.BlockSpec((rows_tile, RADIUS, width - feature), lambda j, p: (0, p[j], 0)),
    ]
    in_specs = [
        pl.BlockSpec((1, rows), lambda j, p: (0, 0)),
        pl.BlockSpec((rows, width), lambda j, p: (0, 0)),
    ]
    operands = [ids.reshape(1, rows), docs]
    aliases = {}
    if prior is not None:
        in_specs += [pl.BlockSpec(memory_space=pl.ANY)] * 2
        operands += list(prior)
        aliases = {3: 0, 4: 1}
    return pl.pallas_call(
        kernel,
        grid_spec=pltpu.PrefetchScalarGridSpec(
            num_scalar_prefetch=1,
            grid=(len(col_blocks),),
            in_specs=in_specs,
            out_specs=out_specs,
        ),
        out_shape=[
            jax.ShapeDtypeStruct((rows_tile, cols_tile, feature), jnp.float32),
            jax.ShapeDtypeStruct((rows_tile, cols_tile, width - feature), jnp.float32),
        ],
        input_output_aliases=aliases,
    )(picks, *operands)


TAPS = [math.exp(-2.0 * k * k / RADIUS**2) for k in range(RADIUS + 1)]
GROUP = 4


def row_group(read, cb_ref, inv_ref, out_ref, first, cols, lanes):
    for c0 in range(0, cols, 8):
        window = [read(j, c0, lanes) for j in range(GROUP + 2 * RADIUS)]
        for q in range(GROUP):
            centre = q + RADIUS
            acc = TAPS[0] * window[centre]
            for k in range(1, RADIUS + 1):
                acc = acc + TAPS[k] * (window[centre - k] + window[centre + k])
            r = first + q
            base = cb_ref[r, pl.ds(c0, 8), lanes].astype(jnp.float32)
            upd = (acc + 8.0 * base) * inv_ref[r, pl.ds(c0, 8), :]
            out_ref[r, pl.ds(c0, 8), lanes] = upd.astype(out_ref.dtype)


def finish_inner(top, middle, bottom, codebook, inv):
    inner, cols, feature = middle.shape
    rows = inner + 2 * RADIUS
    lanes = 128

    def kernel(top_ref, mid_ref, bot_ref, cb_ref, inv_ref, out_ref):
        def read_row(rr, c0):
            if rr < RADIUS:
                return top_ref[rr, pl.ds(c0, 8), :]
            if rr < RADIUS + inner:
                return mid_ref[rr - RADIUS, pl.ds(c0, 8), :]
            return bot_ref[rr - RADIUS - inner, pl.ds(c0, 8), :]

        for first in range(RADIUS, rows - RADIUS, GROUP):

            def read(j, c0, part, first=first):
                return read_row(first + j - RADIUS, c0)

            row_group(read, cb_ref, inv_ref, out_ref, first, cols, slice(None))

    band_spec = pl.BlockSpec((RADIUS, cols, lanes), lambda j: (0, 0, j))
    slab_spec = pl.BlockSpec((rows, cols, lanes), lambda j: (0, 0, j))
    return pl.pallas_call(
        kernel,
        grid=(feature // lanes,),
        in_specs=[
            band_spec,
            pl.BlockSpec((inner, cols, lanes), lambda j: (0, 0, j)),
            band_spec,
            slab_spec,
            pl.BlockSpec((rows, cols, 1), lambda j: (0, 0, 0)),
        ],
        out_specs=slab_spec,
        out_shape=jax.ShapeDtypeStruct(codebook.shape, codebook.dtype),
    )(top, middle, bottom, codebook, inv)


def finish_edges(above, top, middle, bottom, below, codebook, inv, partial):
    rows, cols, feature = codebook.shape
    lanes = 128
    near = 2 * RADIUS
    last_edge = rows // RADIUS - 1
    mid_last = middle.shape[0] // RADIUS - 1

    def kernel(above_ref, top_ref, mid_ref, bot_ref, below_ref, cb_ref, inv_ref, prev_ref, out_ref, ext_ref):
        del prev_ref
        side = pl.program_id(0)

        @pl.when(side == 0)
        def _():
            ext_ref[0:RADIUS] = above_ref[...]
            ext_ref[RADIUS:near] = top_ref[...]
            ext_ref[near:] = mid_ref[...]

        @pl.when(side == 1)
        def _():
            ext_ref[0:RADIUS] = mid_ref[...]
            ext_ref[RADIUS:near] = bot_ref[...]
            ext_ref[near:] = below_ref[...]

        def body(i, carry):
            first = i * GROUP

            def read(j, c0, part):
                return ext_ref[first + j, pl.ds(c0, 8), part]

            for lane in range(0, feature, lanes):
                row_group(read, cb_ref, inv_ref, out_ref, first, cols, pl.ds(lane, lanes))
            return carry

        lax.fori_loop(0, RADIUS // GROUP, body, 0)

    band_spec = pl.BlockSpec((RADIUS, cols, feature), lambda i: (0, 0, 0))
    edge_spec = pl.BlockSpec((RADIUS, cols, feature), lambda i: (i * last_edge, 0, 0))
    return pl.pallas_call(
        kernel,
        grid=(2,),
        in_specs=[
            band_spec,
            band_spec,
            pl.BlockSpec((RADIUS, cols, feature), lambda i: (i * mid_last, 0, 0)),
            band_spec,
            band_spec,
            edge_spec,
            pl.BlockSpec((RADIUS, cols, 1), lambda i: (i, 0, 0)),
            pl.BlockSpec(memory_space=pl.ANY),
        ],
        out_specs=edge_spec,
        out_shape=jax.ShapeDtypeStruct(codebook.shape, codebook.dtype),
        scratch_shapes=[pltpu.VMEM((near + RADIUS, cols, feature), jnp.float32)],
        input_output_aliases={7: 0},
    )(above, top, middle, bottom, below, codebook, inv, partial)


def exchange(lead, last, axis):
    devices = lax.axis_size(axis)
    up = [(i, i + 1) for i in range(devices - 1)]
    down = [(j, i) for i, j in up]
    return lax.ppermute(last, axis, up), lax.ppermute(lead, axis, down)


def on_device(documents, owner_tile, unit_in_tile, codebook):
    rows_mx = lax.axis_size("mx")
    cols_my = lax.axis_size("my")
    tile_total = rows_mx * cols_my
    rows_tile, cols_tile, feature = codebook.shape
    doc_count = documents.shape[0]
    capacity = max(2, 2 * doc_count // tile_total)
    target = owner_tile[:, 0]
    tile_hits = (target[:, None] == jnp.arange(tile_total, dtype=jnp.int32)[None, :]).astype(
        jnp.int32
    )
    earlier = jnp.cumsum(tile_hits, axis=0) - tile_hits
    slot_pos = jnp.sum(earlier * tile_hits, axis=1)
    unit_row = unit_in_tile // cols_tile
    unit_col = unit_in_tile % cols_tile
    extra = jnp.zeros((doc_count, 128), jnp.bfloat16)
    extra = extra.at[:, 0].set(unit_row.astype(jnp.bfloat16))
    extra = extra.at[:, 1].set(unit_col.astype(jnp.bfloat16))
    extra = extra.at[:, 2].set(1.0)
    rows_out = jnp.concatenate([documents, extra], axis=1)
    width = feature + 128
    send_place = target * capacity + slot_pos
    outgoing = jnp.zeros((tile_total * capacity, width), jnp.bfloat16).at[send_place].set(rows_out)
    got = lax.all_to_all(
        outgoing.reshape(tile_total, capacity, width),
        ("mx", "my"),
        split_axis=0,
        concat_axis=0,
        tiled=True,
    ).reshape(-1, width)
    mark_row = got[:, feature].astype(jnp.int32)
    mark_col = got[:, feature + 1].astype(jnp.int32)
    unit_ids = jnp.where(got[:, feature + 2] > 0.5, mark_row * cols_tile + mark_col, -1)
    col_total = cols_tile // RADIUS
    bands = accumulate(unit_ids, got, rows_tile, cols_tile, feature, [0, col_total - 1])
    last = cols_tile - RADIUS
    lead = jnp.concatenate([bands[0][:, :RADIUS], bands[1][:, :RADIUS]], axis=2)
    tail = jnp.concatenate([bands[0][:, last:], bands[1][:, last:]], axis=2)
    from_left, from_right = exchange(lead, tail, "my")
    hits_left, hits_right = from_left[:, :, feature + 2], from_right[:, :, feature + 2]
    from_left, from_right = from_left[:, :, :feature], from_right[:, :, :feature]
    inner = list(range(1, col_total - 1))
    numerator, counter = accumulate(unit_ids, got, rows_tile, cols_tile, feature, inner, bands)
    counter = counter[:, :, 2]

    g_rows = jnp.asarray(band_matrix(rows_tile))
    g_cols = jnp.asarray(band_matrix(cols_tile))
    ext_hits = jnp.concatenate([hits_left, counter, hits_right], axis=1)
    col_hits = jnp.einsum("ck,rk->rc", g_cols, ext_hits, precision=HI)
    last = rows_tile - RADIUS

    def col_pass(lo, hi):
        pieces = [from_left[lo:hi], numerator[lo:hi], from_right[lo:hi]]
        return jnp.einsum("ck,rke->rce", g_cols, jnp.concatenate(pieces, axis=1), precision=HI)

    col_top, col_bottom = col_pass(0, RADIUS), col_pass(last, rows_tile)

    def with_hits(part, rows):
        hit_lanes = jnp.pad(col_hits[rows][:, :, None], ((0, 0), (0, 0), (0, 127)))
        return jnp.concatenate([part, hit_lanes], axis=2)

    above, below = exchange(
        with_hits(col_top, slice(0, RADIUS)),
        with_hits(col_bottom, slice(last, rows_tile)),
        "mx",
    )
    hits_above, hits_below = above[:, :, feature], below[:, :, feature]
    col_mid = col_pass(RADIUS, last)
    inner_hits = jnp.einsum("rk,kc->rc", g_rows[RADIUS:last, RADIUS : RADIUS + rows_tile], col_hits, precision=HI)
    inv_inner = 1.0 / (inner_hits + 8.0)
    inv = jnp.concatenate([jnp.zeros_like(inv_inner[:RADIUS]), inv_inner, jnp.zeros_like(inv_inner[:RADIUS])])
    inv = inv[:, :, None]
    edge_top = jnp.concatenate([hits_above, col_hits[: 2 * RADIUS]], axis=0)
    edge_bottom = jnp.concatenate([col_hits[last - RADIUS :], hits_below], axis=0)
    g_edge = g_rows[:RADIUS, : 3 * RADIUS]
    top_hits = jnp.einsum("rk,kc->rc", g_edge, edge_top, precision=HI)
    bottom_hits = jnp.einsum("rk,kc->rc", g_edge, edge_bottom, precision=HI)
    inv_edges = (1.0 / (jnp.concatenate([top_hits, bottom_hits], axis=0) + 8.0))[:, :, None]
    partial = finish_inner(col_top, col_mid, col_bottom, codebook, inv)
    return finish_edges(above, col_top, col_mid, col_bottom, below, codebook, inv_edges, partial)


def solution(mesh):
    return jax.shard_map(
        on_device,
        mesh=mesh,
        in_specs=(
            P(("mx", "my"), None),
            P(("mx", "my"), None),
            P(("mx", "my")),
            P("mx", "my", None),
        ),
        out_specs=P("mx", "my", None),
        check_vma=False,
    )
```

```python
import math

import jax
import jax.numpy as jnp
import numpy as np
from jax import lax
from jax.experimental import pallas as pl
from jax.experimental.pallas import tpu as pltpu
from jax.sharding import PartitionSpec as P

RADIUS = 8
HI = lax.Precision.HIGH


def band_matrix(out_len):
    ext = out_len + 2 * RADIUS
    mat = np.zeros((out_len, ext), np.float32)
    for r in range(out_len):
        for k in range(-RADIUS, RADIUS + 1):
            mat[r, r + k + RADIUS] = math.exp(-2.0 * k * k / RADIUS**2)
    return mat


def accumulate(ids, docs, rows_tile, cols_tile, feature, col_blocks, prior=None):
    rows, width = docs.shape
    band = rows_tile * RADIUS
    picks = jnp.asarray(col_blocks, jnp.int32)

    def kernel(picks_ref, ids_ref, docs_ref, *refs):
        num_ref, hits_ref = refs[-2:]
        place = lax.broadcasted_iota(jnp.int32, (band, rows), 0)
        first_col = picks_ref[pl.program_id(0)] * RADIUS
        units = (place // RADIUS) * cols_tile + first_col + place % RADIUS
        one_hot = (units == ids_ref[...]).astype(jnp.bfloat16)
        sums = jnp.dot(one_hot, docs_ref[...], preferred_element_type=jnp.float32)
        num_ref[...] = sums[:, :feature].reshape(rows_tile, RADIUS, feature)
        hits_ref[...] = sums[:, feature:].reshape(rows_tile, RADIUS, width - feature)

    out_specs = [
        pl.BlockSpec((rows_tile, RADIUS, feature), lambda j, p: (0, p[j], 0)),
        pl.BlockSpec((rows_tile, RADIUS, width - feature), lambda j, p: (0, p[j], 0)),
    ]
    in_specs = [
        pl.BlockSpec((1, rows), lambda j, p: (0, 0)),
        pl.BlockSpec((rows, width), lambda j, p: (0, 0)),
    ]
    operands = [ids.reshape(1, rows), docs]
    aliases = {}
    if prior is not None:
        in_specs += [pl.BlockSpec(memory_space=pl.ANY)] * 2
        operands += list(prior)
        aliases = {3: 0, 4: 1}
    return pl.pallas_call(
        kernel,
        grid_spec=pltpu.PrefetchScalarGridSpec(
            num_scalar_prefetch=1,
            grid=(len(col_blocks),),
            in_specs=in_specs,
            out_specs=out_specs,
        ),
        out_shape=[
            jax.ShapeDtypeStruct((rows_tile, cols_tile, feature), jnp.float32),
            jax.ShapeDtypeStruct((rows_tile, cols_tile, width - feature), jnp.float32),
        ],
        input_output_aliases=aliases,
    )(picks, *operands)


TAPS = [math.exp(-2.0 * k * k / RADIUS**2) for k in range(RADIUS + 1)]
GROUP = 4


def row_group(read, cb_ref, inv_ref, out_ref, first, cols, lanes):
    for c0 in range(0, cols, 8):
        window = [read(j, c0, lanes) for j in range(GROUP + 2 * RADIUS)]
        for q in range(GROUP):
            centre = q + RADIUS
            acc = TAPS[0] * window[centre]
            for k in range(1, RADIUS + 1):
                acc = acc + TAPS[k] * (window[centre - k] + window[centre + k])
            r = first + q
            base = cb_ref[r, pl.ds(c0, 8), lanes].astype(jnp.float32)
            upd = (acc + 8.0 * base) * inv_ref[r, pl.ds(c0, 8), :]
            out_ref[r, pl.ds(c0, 8), lanes] = upd.astype(out_ref.dtype)


def finish_inner(middle, codebook, inv):
    rows, cols, feature = middle.shape
    lanes = 128

    def kernel(mid_ref, cb_ref, inv_ref, out_ref):
        def body(i, carry):
            first = RADIUS + i * GROUP

            def read(j, c0, part):
                return mid_ref[first + j - RADIUS, pl.ds(c0, 8), part]

            row_group(read, cb_ref, inv_ref, out_ref, first, cols, slice(None))
            return carry

        lax.fori_loop(0, (rows - 2 * RADIUS) // GROUP, body, 0)

    slab_spec = pl.BlockSpec((rows, cols, lanes), lambda j: (0, 0, j))
    return pl.pallas_call(
        kernel,
        grid=(feature // lanes,),
        in_specs=[slab_spec, slab_spec, pl.BlockSpec((rows, cols, 1), lambda j: (0, 0, 0))],
        out_specs=slab_spec,
        out_shape=jax.ShapeDtypeStruct(codebook.shape, codebook.dtype),
    )(middle, codebook, inv)


def finish_edges(above, middle, below, codebook, inv, partial):
    rows, cols, feature = middle.shape
    lanes = 128
    near = 2 * RADIUS
    last_edge = rows // RADIUS - 1

    def kernel(above_ref, mid_ref, below_ref, cb_ref, inv_ref, prev_ref, out_ref, ext_ref):
        del prev_ref
        side = pl.program_id(0)

        @pl.when(side == 0)
        def _():
            ext_ref[0:RADIUS] = above_ref[...]
            ext_ref[RADIUS:] = mid_ref[...]

        @pl.when(side == 1)
        def _():
            ext_ref[0:near] = mid_ref[...]
            ext_ref[near:] = below_ref[...]

        def body(i, carry):
            first = i * GROUP

            def read(j, c0, part):
                return ext_ref[first + j, pl.ds(c0, 8), part]

            for lane in range(0, feature, lanes):
                row_group(read, cb_ref, inv_ref, out_ref, first, cols, pl.ds(lane, lanes))
            return carry

        lax.fori_loop(0, RADIUS // GROUP, body, 0)

    halo_spec = pl.BlockSpec((RADIUS, cols, feature), lambda i: (0, 0, 0))
    edge_spec = pl.BlockSpec((RADIUS, cols, feature), lambda i: (i * last_edge, 0, 0))
    return pl.pallas_call(
        kernel,
        grid=(2,),
        in_specs=[
            halo_spec,
            pl.BlockSpec((near, cols, feature), lambda i: (i * (rows // near - 1), 0, 0)),
            halo_spec,
            edge_spec,
            pl.BlockSpec((RADIUS, cols, 1), lambda i: (i, 0, 0)),
            pl.BlockSpec(memory_space=pl.ANY),
        ],
        out_specs=edge_spec,
        out_shape=jax.ShapeDtypeStruct(codebook.shape, codebook.dtype),
        scratch_shapes=[pltpu.VMEM((near + RADIUS, cols, feature), jnp.float32)],
        input_output_aliases={5: 0},
    )(above, middle, below, codebook, inv, partial)


def exchange(lead, last, axis):
    devices = lax.axis_size(axis)
    up = [(i, i + 1) for i in range(devices - 1)]
    down = [(j, i) for i, j in up]
    return lax.ppermute(last, axis, up), lax.ppermute(lead, axis, down)


def on_device(documents, owner_tile, unit_in_tile, codebook):
    rows_mx = lax.axis_size("mx")
    cols_my = lax.axis_size("my")
    tile_total = rows_mx * cols_my
    rows_tile, cols_tile, feature = codebook.shape
    doc_count = documents.shape[0]
    capacity = max(2, 2 * doc_count // tile_total)
    target = owner_tile[:, 0]
    tile_hits = (target[:, None] == jnp.arange(tile_total, dtype=jnp.int32)[None, :]).astype(
        jnp.int32
    )
    earlier = jnp.cumsum(tile_hits, axis=0) - tile_hits
    slot_pos = jnp.sum(earlier * tile_hits, axis=1)
    unit_row = unit_in_tile // cols_tile
    unit_col = unit_in_tile % cols_tile
    extra = jnp.zeros((doc_count, 128), jnp.bfloat16)
    extra = extra.at[:, 0].set(unit_row.astype(jnp.bfloat16))
    extra = extra.at[:, 1].set(unit_col.astype(jnp.bfloat16))
    extra = extra.at[:, 2].set(1.0)
    rows_out = jnp.concatenate([documents, extra], axis=1)
    width = feature + 128
    send_place = target * capacity + slot_pos
    outgoing = jnp.zeros((tile_total * capacity, width), jnp.bfloat16).at[send_place].set(rows_out)
    got = lax.all_to_all(
        outgoing.reshape(tile_total, capacity, width),
        ("mx", "my"),
        split_axis=0,
        concat_axis=0,
        tiled=True,
    ).reshape(-1, width)
    mark_row = got[:, feature].astype(jnp.int32)
    mark_col = got[:, feature + 1].astype(jnp.int32)
    unit_ids = jnp.where(got[:, feature + 2] > 0.5, mark_row * cols_tile + mark_col, -1)
    col_total = cols_tile // RADIUS
    bands = accumulate(unit_ids, got, rows_tile, cols_tile, feature, [0, col_total - 1])
    last = cols_tile - RADIUS
    lead = jnp.concatenate([bands[0][:, :RADIUS], bands[1][:, :RADIUS]], axis=2)
    tail = jnp.concatenate([bands[0][:, last:], bands[1][:, last:]], axis=2)
    from_left, from_right = exchange(lead, tail, "my")
    hits_left, hits_right = from_left[:, :, feature + 2], from_right[:, :, feature + 2]
    from_left, from_right = from_left[:, :, :feature], from_right[:, :, :feature]
    inner = list(range(1, col_total - 1))
    numerator, counter = accumulate(unit_ids, got, rows_tile, cols_tile, feature, inner, bands)
    counter = counter[:, :, 2]

    g_rows = jnp.asarray(band_matrix(rows_tile))
    g_cols = jnp.asarray(band_matrix(cols_tile))
    ext_hits = jnp.concatenate([hits_left, counter, hits_right], axis=1)
    col_hits = jnp.einsum("ck,rk->rc", g_cols, ext_hits, precision=HI)
    last = rows_tile - RADIUS

    def col_pass(lo, hi):
        pieces = [from_left[lo:hi], numerator[lo:hi], from_right[lo:hi]]
        return jnp.einsum("ck,rke->rce", g_cols, jnp.concatenate(pieces, axis=1), precision=HI)

    col_top, col_bottom = col_pass(0, RADIUS), col_pass(last, rows_tile)

    def with_hits(part, rows):
        hit_lanes = jnp.pad(col_hits[rows][:, :, None], ((0, 0), (0, 0), (0, 127)))
        return jnp.concatenate([part, hit_lanes], axis=2)

    above, below = exchange(
        with_hits(col_top, slice(0, RADIUS)),
        with_hits(col_bottom, slice(last, rows_tile)),
        "mx",
    )
    hits_above, hits_below = above[:, :, feature], below[:, :, feature]
    col_num = col_pass(0, rows_tile)
    inner_hits = jnp.einsum("rk,kc->rc", g_rows[RADIUS:last, RADIUS : RADIUS + rows_tile], col_hits, precision=HI)
    inv_inner = 1.0 / (inner_hits + 8.0)
    inv = jnp.concatenate([jnp.zeros_like(inv_inner[:RADIUS]), inv_inner, jnp.zeros_like(inv_inner[:RADIUS])])
    inv = inv[:, :, None]
    edge_top = jnp.concatenate([hits_above, col_hits[: 2 * RADIUS]], axis=0)
    edge_bottom = jnp.concatenate([col_hits[last - RADIUS :], hits_below], axis=0)
    g_edge = g_rows[:RADIUS, : 3 * RADIUS]
    top_hits = jnp.einsum("rk,kc->rc", g_edge, edge_top, precision=HI)
    bottom_hits = jnp.einsum("rk,kc->rc", g_edge, edge_bottom, precision=HI)
    inv_edges = (1.0 / (jnp.concatenate([top_hits, bottom_hits], axis=0) + 8.0))[:, :, None]
    partial = finish_inner(col_num, codebook, inv)
    return finish_edges(above, col_num, below, codebook, inv_edges, partial)


def solution(mesh):
    return jax.shard_map(
        on_device,
        mesh=mesh,
        in_specs=(
            P(("mx", "my"), None),
            P(("mx", "my"), None),
            P(("mx", "my")),
            P("mx", "my", None),
        ),
        out_specs=P("mx", "my", None),
        check_vma=False,
    )
```

```python
import math

import jax
import jax.numpy as jnp
import numpy as np
from jax import lax
from jax.experimental import pallas as pl
from jax.experimental.pallas import tpu as pltpu
from jax.sharding import PartitionSpec as P

RADIUS = 8
HI = lax.Precision.HIGH


def band_matrix(out_len):
    ext = out_len + 2 * RADIUS
    mat = np.zeros((out_len, ext), np.float32)
    for r in range(out_len):
        for k in range(-RADIUS, RADIUS + 1):
            mat[r, r + k + RADIUS] = math.exp(-2.0 * k * k / RADIUS**2)
    return mat


def accumulate(ids, docs, rows_tile, cols_tile, feature, col_blocks, prior=None):
    rows, width = docs.shape
    band = rows_tile * RADIUS
    picks = jnp.asarray(col_blocks, jnp.int32)

    def kernel(picks_ref, ids_ref, docs_ref, *refs):
        num_ref = refs[-1]
        place = lax.broadcasted_iota(jnp.int32, (band, rows), 0)
        first_col = picks_ref[pl.program_id(0)] * RADIUS
        units = (place // RADIUS) * cols_tile + first_col + place % RADIUS
        one_hot = (units == ids_ref[...]).astype(jnp.bfloat16)
        sums = jnp.dot(one_hot, docs_ref[...], preferred_element_type=jnp.float32)
        num_ref[...] = sums.reshape(rows_tile, RADIUS, width)

    out_specs = pl.BlockSpec((rows_tile, RADIUS, width), lambda j, p: (0, p[j], 0))
    in_specs = [
        pl.BlockSpec((1, rows), lambda j, p: (0, 0)),
        pl.BlockSpec((rows, width), lambda j, p: (0, 0)),
    ]
    operands = [ids.reshape(1, rows), docs]
    aliases = {}
    if prior is not None:
        in_specs += [pl.BlockSpec(memory_space=pl.ANY)]
        operands += [prior]
        aliases = {3: 0}
    return pl.pallas_call(
        kernel,
        grid_spec=pltpu.PrefetchScalarGridSpec(
            num_scalar_prefetch=1,
            grid=(len(col_blocks),),
            in_specs=in_specs,
            out_specs=out_specs,
        ),
        out_shape=jax.ShapeDtypeStruct((rows_tile, cols_tile, width), jnp.float32),
        input_output_aliases=aliases,
    )(picks, *operands)


TAPS = [math.exp(-2.0 * k * k / RADIUS**2) for k in range(RADIUS + 1)]
GROUP = 4


def row_group(read, cb_ref, inv_ref, out_ref, first, cols, lanes):
    for c0 in range(0, cols, 8):
        window = [read(j, c0, lanes) for j in range(GROUP + 2 * RADIUS)]
        for q in range(GROUP):
            centre = q + RADIUS
            acc = TAPS[0] * window[centre]
            for k in range(1, RADIUS + 1):
                acc = acc + TAPS[k] * (window[centre - k] + window[centre + k])
            r = first + q
            base = cb_ref[r, pl.ds(c0, 8), lanes].astype(jnp.float32)
            upd = (acc + 8.0 * base) * inv_ref[r, pl.ds(c0, 8), :]
            out_ref[r, pl.ds(c0, 8), lanes] = upd.astype(out_ref.dtype)


def finish_inner(middle, codebook, inv):
    rows, cols, feature = codebook.shape
    lanes = 128

    def kernel(mid_ref, cb_ref, inv_ref, out_ref):
        def body(i, carry):
            first = RADIUS + i * GROUP

            def read(j, c0, part):
                return mid_ref[first + j - RADIUS, pl.ds(c0, 8), part]

            row_group(read, cb_ref, inv_ref, out_ref, first, cols, slice(None))
            return carry

        lax.fori_loop(0, (rows - 2 * RADIUS) // GROUP, body, 0)

    slab_spec = pl.BlockSpec((rows, cols, lanes), lambda j: (0, 0, j))
    return pl.pallas_call(
        kernel,
        grid=(feature // lanes,),
        in_specs=[slab_spec, slab_spec, pl.BlockSpec((rows, cols, 1), lambda j: (0, 0, 0))],
        out_specs=slab_spec,
        out_shape=jax.ShapeDtypeStruct(codebook.shape, codebook.dtype),
    )(middle, codebook, inv)


def finish_edges(above, middle, below, codebook, inv, partial):
    rows, cols, feature = codebook.shape
    lanes = 128
    near = 2 * RADIUS
    last_edge = rows // RADIUS - 1

    def kernel(above_ref, mid_ref, below_ref, cb_ref, inv_ref, prev_ref, out_ref, ext_ref):
        del prev_ref
        side = pl.program_id(0)

        @pl.when(side == 0)
        def _():
            ext_ref[0:RADIUS] = above_ref[...]
            ext_ref[RADIUS:] = mid_ref[...]

        @pl.when(side == 1)
        def _():
            ext_ref[0:near] = mid_ref[...]
            ext_ref[near:] = below_ref[...]

        def body(i, carry):
            first = i * GROUP

            def read(j, c0, part):
                return ext_ref[first + j, pl.ds(c0, 8), part]

            for lane in range(0, feature, lanes):
                row_group(read, cb_ref, inv_ref, out_ref, first, cols, pl.ds(lane, lanes))
            return carry

        lax.fori_loop(0, RADIUS // GROUP, body, 0)

    halo_spec = pl.BlockSpec((RADIUS, cols, feature), lambda i: (0, 0, 0))
    edge_spec = pl.BlockSpec((RADIUS, cols, feature), lambda i: (i * last_edge, 0, 0))
    return pl.pallas_call(
        kernel,
        grid=(2,),
        in_specs=[
            halo_spec,
            pl.BlockSpec((near, cols, feature), lambda i: (i * (rows // near - 1), 0, 0)),
            halo_spec,
            edge_spec,
            pl.BlockSpec((RADIUS, cols, 1), lambda i: (i, 0, 0)),
            pl.BlockSpec(memory_space=pl.ANY),
        ],
        out_specs=edge_spec,
        out_shape=jax.ShapeDtypeStruct(codebook.shape, codebook.dtype),
        scratch_shapes=[pltpu.VMEM((near + RADIUS, cols, feature), jnp.float32)],
        input_output_aliases={5: 0},
    )(above, middle, below, codebook, inv, partial)


def exchange(lead, last, axis):
    devices = lax.axis_size(axis)
    up = [(i, i + 1) for i in range(devices - 1)]
    down = [(j, i) for i, j in up]
    return lax.ppermute(last, axis, up), lax.ppermute(lead, axis, down)


def on_device(documents, owner_tile, unit_in_tile, codebook):
    rows_mx = lax.axis_size("mx")
    cols_my = lax.axis_size("my")
    tile_total = rows_mx * cols_my
    rows_tile, cols_tile, feature = codebook.shape
    doc_count = documents.shape[0]
    capacity = max(2, 2 * doc_count // tile_total)
    target = owner_tile[:, 0]
    tile_hits = (target[:, None] == jnp.arange(tile_total, dtype=jnp.int32)[None, :]).astype(
        jnp.int32
    )
    earlier = jnp.cumsum(tile_hits, axis=0) - tile_hits
    slot_pos = jnp.sum(earlier * tile_hits, axis=1)
    unit_row = unit_in_tile // cols_tile
    unit_col = unit_in_tile % cols_tile
    extra = jnp.zeros((doc_count, 128), jnp.bfloat16)
    extra = extra.at[:, 0].set(unit_row.astype(jnp.bfloat16))
    extra = extra.at[:, 1].set(unit_col.astype(jnp.bfloat16))
    extra = extra.at[:, 2].set(1.0)
    rows_out = jnp.concatenate([documents, extra], axis=1)
    width = feature + 128
    send_place = target * capacity + slot_pos
    outgoing = jnp.zeros((tile_total * capacity, width), jnp.bfloat16).at[send_place].set(rows_out)
    got = lax.all_to_all(
        outgoing.reshape(tile_total, capacity, width),
        ("mx", "my"),
        split_axis=0,
        concat_axis=0,
        tiled=True,
    ).reshape(-1, width)
    mark_row = got[:, feature].astype(jnp.int32)
    mark_col = got[:, feature + 1].astype(jnp.int32)
    unit_ids = jnp.where(got[:, feature + 2] > 0.5, mark_row * cols_tile + mark_col, -1)
    col_total = cols_tile // RADIUS
    bands = accumulate(unit_ids, got, rows_tile, cols_tile, feature, [0, col_total - 1])
    last = cols_tile - RADIUS
    from_left, from_right = exchange(bands[:, :RADIUS], bands[:, last:], "my")
    inner = list(range(1, col_total - 1))
    numerator = accumulate(unit_ids, got, rows_tile, cols_tile, feature, inner, bands)

    g_rows = jnp.asarray(band_matrix(rows_tile))
    g_cols = jnp.asarray(band_matrix(cols_tile))
    last = rows_tile - RADIUS

    def col_pass(lo, hi):
        pieces = [from_left[lo:hi], numerator[lo:hi], from_right[lo:hi]]
        return jnp.einsum("ck,rke->rce", g_cols, jnp.concatenate(pieces, axis=1), precision=HI)

    col_top, col_bottom = col_pass(0, RADIUS), col_pass(last, rows_tile)

    above, below = exchange(col_top, col_bottom, "mx")
    hits_above, hits_below = above[:, :, feature + 2], below[:, :, feature + 2]
    col_num = col_pass(0, rows_tile)
    col_hits = col_num[:, :, feature + 2]
    inner_hits = jnp.einsum("rk,kc->rc", g_rows[RADIUS:last, RADIUS : RADIUS + rows_tile], col_hits, precision=HI)
    inv_inner = 1.0 / (inner_hits + 8.0)
    inv = jnp.concatenate([jnp.zeros_like(inv_inner[:RADIUS]), inv_inner, jnp.zeros_like(inv_inner[:RADIUS])])
    inv = inv[:, :, None]
    edge_top = jnp.concatenate([hits_above, col_hits[: 2 * RADIUS]], axis=0)
    edge_bottom = jnp.concatenate([col_hits[last - RADIUS :], hits_below], axis=0)
    g_edge = g_rows[:RADIUS, : 3 * RADIUS]
    top_hits = jnp.einsum("rk,kc->rc", g_edge, edge_top, precision=HI)
    bottom_hits = jnp.einsum("rk,kc->rc", g_edge, edge_bottom, precision=HI)
    inv_edges = (1.0 / (jnp.concatenate([top_hits, bottom_hits], axis=0) + 8.0))[:, :, None]
    partial = finish_inner(col_num, codebook, inv)
    return finish_edges(above, col_num, below, codebook, inv_edges, partial)


def solution(mesh):
    return jax.shard_map(
        on_device,
        mesh=mesh,
        in_specs=(
            P(("mx", "my"), None),
            P(("mx", "my"), None),
            P(("mx", "my")),
            P("mx", "my", None),
        ),
        out_specs=P("mx", "my", None),
        check_vma=False,
    )
```

```python
import math

import jax
import jax.numpy as jnp
import numpy as np
from jax import lax
from jax.experimental import pallas as pl
from jax.experimental.pallas import tpu as pltpu
from jax.sharding import PartitionSpec as P

RADIUS = 8
HI = lax.Precision.HIGH


def band_matrix(out_len):
    ext = out_len + 2 * RADIUS
    mat = np.zeros((out_len, ext), np.float32)
    for r in range(out_len):
        for k in range(-RADIUS, RADIUS + 1):
            mat[r, r + k + RADIUS] = math.exp(-2.0 * k * k / RADIUS**2)
    return mat


def accumulate(ids, docs, rows_tile, cols_tile, feature, col_blocks, prior=None):
    rows, width = docs.shape
    band = rows_tile * RADIUS
    picks = jnp.asarray(col_blocks, jnp.int32)

    def kernel(picks_ref, ids_ref, docs_ref, *refs):
        num_ref = refs[-1] if prior is not None else refs[-3]
        place = lax.broadcasted_iota(jnp.int32, (band, rows), 0)
        first_col = picks_ref[pl.program_id(0)] * RADIUS
        units = (place // RADIUS) * cols_tile + first_col + place % RADIUS
        one_hot = (units == ids_ref[...]).astype(jnp.bfloat16)
        sums = jnp.dot(one_hot, docs_ref[...], preferred_element_type=jnp.float32)
        num_ref[...] = sums.reshape(rows_tile, RADIUS, width)
        if prior is None:
            for side in range(2):

                @pl.when(pl.program_id(0) == side)
                def _():
                    refs[side - 2][...] = sums.reshape(rows_tile, RADIUS, width)

    out_specs = [pl.BlockSpec((rows_tile, RADIUS, width), lambda j, p: (0, p[j], 0))]
    out_shape = [jax.ShapeDtypeStruct((rows_tile, cols_tile, width), jnp.float32)]
    if prior is None:
        out_specs += [pl.BlockSpec((rows_tile, RADIUS, width), lambda j, p: (0, 0, 0))] * 2
        out_shape += [jax.ShapeDtypeStruct((rows_tile, RADIUS, width), jnp.float32)] * 2
    in_specs = [
        pl.BlockSpec((1, rows), lambda j, p: (0, 0)),
        pl.BlockSpec((rows, width), lambda j, p: (0, 0)),
    ]
    operands = [ids.reshape(1, rows), docs]
    aliases = {}
    if prior is not None:
        in_specs += [pl.BlockSpec(memory_space=pl.ANY)]
        operands += [prior]
        aliases = {3: 0}
    return pl.pallas_call(
        kernel,
        grid_spec=pltpu.PrefetchScalarGridSpec(
            num_scalar_prefetch=1,
            grid=(len(col_blocks),),
            in_specs=in_specs,
            out_specs=out_specs,
        ),
        out_shape=out_shape,
        input_output_aliases=aliases,
    )(picks, *operands)


TAPS = [math.exp(-2.0 * k * k / RADIUS**2) for k in range(RADIUS + 1)]
GROUP = 4


def row_group(read, cb_ref, inv_ref, out_ref, first, cols, lanes):
    for c0 in range(0, cols, 8):
        window = [read(j, c0, lanes) for j in range(GROUP + 2 * RADIUS)]
        for q in range(GROUP):
            centre = q + RADIUS
            acc = TAPS[0] * window[centre]
            for k in range(1, RADIUS + 1):
                acc = acc + TAPS[k] * (window[centre - k] + window[centre + k])
            r = first + q
            base = cb_ref[r, pl.ds(c0, 8), lanes].astype(jnp.float32)
            upd = (acc + 8.0 * base) * inv_ref[r, pl.ds(c0, 8), :]
            out_ref[r, pl.ds(c0, 8), lanes] = upd.astype(out_ref.dtype)


def finish_inner(middle, codebook, inv):
    rows, cols, feature = codebook.shape
    lanes = 128

    def kernel(mid_ref, cb_ref, inv_ref, out_ref):
        def body(i, carry):
            first = RADIUS + i * GROUP

            def read(j, c0, part):
                return mid_ref[first + j - RADIUS, pl.ds(c0, 8), part]

            row_group(read, cb_ref, inv_ref, out_ref, first, cols, slice(None))
            return carry

        lax.fori_loop(0, (rows - 2 * RADIUS) // GROUP, body, 0)

    slab_spec = pl.BlockSpec((rows, cols, lanes), lambda j: (0, 0, j))
    return pl.pallas_call(
        kernel,
        grid=(feature // lanes,),
        in_specs=[slab_spec, slab_spec, pl.BlockSpec((rows, cols, 1), lambda j: (0, 0, 0))],
        out_specs=slab_spec,
        out_shape=jax.ShapeDtypeStruct(codebook.shape, codebook.dtype),
    )(middle, codebook, inv)


def finish_edges(above, middle, below, codebook, inv, partial):
    rows, cols, feature = codebook.shape
    lanes = 128
    near = 2 * RADIUS
    last_edge = rows // RADIUS - 1

    def kernel(above_ref, mid_ref, below_ref, cb_ref, inv_ref, prev_ref, out_ref, ext_ref):
        del prev_ref
        side = pl.program_id(0)

        @pl.when(side == 0)
        def _():
            ext_ref[0:RADIUS] = above_ref[...]
            ext_ref[RADIUS:] = mid_ref[...]

        @pl.when(side == 1)
        def _():
            ext_ref[0:near] = mid_ref[...]
            ext_ref[near:] = below_ref[...]

        def body(i, carry):
            first = i * GROUP

            def read(j, c0, part):
                return ext_ref[first + j, pl.ds(c0, 8), part]

            for lane in range(0, feature, lanes):
                row_group(read, cb_ref, inv_ref, out_ref, first, cols, pl.ds(lane, lanes))
            return carry

        lax.fori_loop(0, RADIUS // GROUP, body, 0)

    halo_spec = pl.BlockSpec((RADIUS, cols, feature), lambda i: (0, 0, 0))
    edge_spec = pl.BlockSpec((RADIUS, cols, feature), lambda i: (i * last_edge, 0, 0))
    return pl.pallas_call(
        kernel,
        grid=(2,),
        in_specs=[
            halo_spec,
            pl.BlockSpec((near, cols, feature), lambda i: (i * (rows // near - 1), 0, 0)),
            halo_spec,
            edge_spec,
            pl.BlockSpec((RADIUS, cols, 1), lambda i: (i, 0, 0)),
            pl.BlockSpec(memory_space=pl.ANY),
        ],
        out_specs=edge_spec,
        out_shape=jax.ShapeDtypeStruct(codebook.shape, codebook.dtype),
        scratch_shapes=[pltpu.VMEM((near + RADIUS, cols, feature), jnp.float32)],
        input_output_aliases={5: 0},
    )(above, middle, below, codebook, inv, partial)


def exchange(lead, last, axis):
    devices = lax.axis_size(axis)
    up = [(i, i + 1) for i in range(devices - 1)]
    down = [(j, i) for i, j in up]
    return lax.ppermute(last, axis, up), lax.ppermute(lead, axis, down)


def on_device(documents, owner_tile, unit_in_tile, codebook):
    rows_mx = lax.axis_size("mx")
    cols_my = lax.axis_size("my")
    tile_total = rows_mx * cols_my
    rows_tile, cols_tile, feature = codebook.shape
    doc_count = documents.shape[0]
    capacity = max(2, 2 * doc_count // tile_total)
    target = owner_tile[:, 0]
    tile_hits = (target[:, None] == jnp.arange(tile_total, dtype=jnp.int32)[None, :]).astype(
        jnp.int32
    )
    earlier = jnp.cumsum(tile_hits, axis=0) - tile_hits
    slot_pos = jnp.sum(earlier * tile_hits, axis=1)
    unit_row = unit_in_tile // cols_tile
    unit_col = unit_in_tile % cols_tile
    extra = jnp.zeros((doc_count, 128), jnp.bfloat16)
    extra = extra.at[:, 0].set(unit_row.astype(jnp.bfloat16))
    extra = extra.at[:, 1].set(unit_col.astype(jnp.bfloat16))
    extra = extra.at[:, 2].set(1.0)
    rows_out = jnp.concatenate([documents, extra], axis=1)
    width = feature + 128
    send_place = target * capacity + slot_pos
    outgoing = jnp.zeros((tile_total * capacity, width), jnp.bfloat16).at[send_place].set(rows_out)
    got = lax.all_to_all(
        outgoing.reshape(tile_total, capacity, width),
        ("mx", "my"),
        split_axis=0,
        concat_axis=0,
        tiled=True,
    ).reshape(-1, width)
    mark_row = got[:, feature].astype(jnp.int32)
    mark_col = got[:, feature + 1].astype(jnp.int32)
    unit_ids = jnp.where(got[:, feature + 2] > 0.5, mark_row * cols_tile + mark_col, -1)
    col_total = cols_tile // RADIUS
    bands = accumulate(unit_ids, got, rows_tile, cols_tile, feature, [0, col_total - 1])
    last = cols_tile - RADIUS
    bands, lead, tail = bands
    from_left, from_right = exchange(lead, tail, "my")
    inner = list(range(1, col_total - 1))
    (numerator,) = accumulate(unit_ids, got, rows_tile, cols_tile, feature, inner, bands)

    g_rows = jnp.asarray(band_matrix(rows_tile))
    g_cols = jnp.asarray(band_matrix(cols_tile))
    last = rows_tile - RADIUS

    def col_pass(lo, hi):
        pieces = [from_left[lo:hi], numerator[lo:hi], from_right[lo:hi]]
        return jnp.einsum("ck,rke->rce", g_cols, jnp.concatenate(pieces, axis=1), precision=HI)

    col_top, col_bottom = col_pass(0, RADIUS), col_pass(last, rows_tile)

    above, below = exchange(col_top, col_bottom, "mx")
    hits_above, hits_below = above[:, :, feature + 2], below[:, :, feature + 2]
    col_num = col_pass(0, rows_tile)
    col_hits = col_num[:, :, feature + 2]
    inner_hits = jnp.einsum("rk,kc->rc", g_rows[RADIUS:last, RADIUS : RADIUS + rows_tile], col_hits, precision=HI)
    inv_inner = 1.0 / (inner_hits + 8.0)
    inv = jnp.concatenate([jnp.zeros_like(inv_inner[:RADIUS]), inv_inner, jnp.zeros_like(inv_inner[:RADIUS])])
    inv = inv[:, :, None]
    edge_top = jnp.concatenate([hits_above, col_hits[: 2 * RADIUS]], axis=0)
    edge_bottom = jnp.concatenate([col_hits[last - RADIUS :], hits_below], axis=0)
    g_edge = g_rows[:RADIUS, : 3 * RADIUS]
    top_hits = jnp.einsum("rk,kc->rc", g_edge, edge_top, precision=HI)
    bottom_hits = jnp.einsum("rk,kc->rc", g_edge, edge_bottom, precision=HI)
    inv_edges = (1.0 / (jnp.concatenate([top_hits, bottom_hits], axis=0) + 8.0))[:, :, None]
    partial = finish_inner(col_num, codebook, inv)
    return finish_edges(above, col_num, below, codebook, inv_edges, partial)


def solution(mesh):
    return jax.shard_map(
        on_device,
        mesh=mesh,
        in_specs=(
            P(("mx", "my"), None),
            P(("mx", "my"), None),
            P(("mx", "my")),
            P("mx", "my", None),
        ),
        out_specs=P("mx", "my", None),
        check_vma=False,
    )
```

```python
import math

import jax
import jax.numpy as jnp
import numpy as np
from jax import lax
from jax.experimental import pallas as pl
from jax.experimental.pallas import tpu as pltpu
from jax.sharding import PartitionSpec as P

RADIUS = 8
HI = lax.Precision.HIGH


def band_matrix(out_len):
    ext = out_len + 2 * RADIUS
    mat = np.zeros((out_len, ext), np.float32)
    for r in range(out_len):
        for k in range(-RADIUS, RADIUS + 1):
            mat[r, r + k + RADIUS] = math.exp(-2.0 * k * k / RADIUS**2)
    return mat


def accumulate(ids, docs, rows_tile, cols_tile, feature, col_blocks, prior=None):
    rows, width = docs.shape
    band = rows_tile * RADIUS
    picks = jnp.asarray(col_blocks, jnp.int32)

    def kernel(picks_ref, ids_ref, docs_ref, *refs):
        num_ref = refs[-1] if prior is not None else refs[-3]
        place = lax.broadcasted_iota(jnp.int32, (band, rows), 0)
        first_col = picks_ref[pl.program_id(0)] * RADIUS
        units = (place // RADIUS) * cols_tile + first_col + place % RADIUS
        one_hot = (units == ids_ref[...]).astype(jnp.bfloat16)
        sums = jnp.dot(one_hot, docs_ref[...], preferred_element_type=jnp.float32)
        num_ref[...] = sums.reshape(rows_tile, RADIUS, width)
        if prior is None:
            for side in range(2):

                @pl.when(pl.program_id(0) == side)
                def _():
                    refs[side - 2][...] = sums.reshape(rows_tile, RADIUS, width)

    out_specs = [pl.BlockSpec((rows_tile, RADIUS, width), lambda j, p: (0, p[j], 0))]
    out_shape = [jax.ShapeDtypeStruct((rows_tile, cols_tile, width), jnp.float32)]
    if prior is None:
        out_specs += [pl.BlockSpec((rows_tile, RADIUS, width), lambda j, p: (0, 0, 0))] * 2
        out_shape += [jax.ShapeDtypeStruct((rows_tile, RADIUS, width), jnp.float32)] * 2
    in_specs = [
        pl.BlockSpec((1, rows), lambda j, p: (0, 0)),
        pl.BlockSpec((rows, width), lambda j, p: (0, 0)),
    ]
    operands = [ids.reshape(1, rows), docs]
    aliases = {}
    if prior is not None:
        in_specs += [pl.BlockSpec(memory_space=pl.ANY)]
        operands += [prior]
        aliases = {3: 0}
    return pl.pallas_call(
        kernel,
        grid_spec=pltpu.PrefetchScalarGridSpec(
            num_scalar_prefetch=1,
            grid=(len(col_blocks),),
            in_specs=in_specs,
            out_specs=out_specs,
        ),
        out_shape=out_shape,
        input_output_aliases=aliases,
    )(picks, *operands)


TAPS = [math.exp(-2.0 * k * k / RADIUS**2) for k in range(RADIUS + 1)]
GROUP = 4


def row_group(read, first, cols, lanes, emit):
    for c0 in range(0, cols, 8):
        window = [read(j, c0, lanes) for j in range(GROUP + 2 * RADIUS)]
        for q in range(GROUP):
            centre = q + RADIUS
            acc = TAPS[0] * window[centre]
            for k in range(1, RADIUS + 1):
                acc = acc + TAPS[k] * (window[centre - k] + window[centre + k])
            emit(first + q, c0, acc)


def updater(cb_ref, inv_ref, out_ref, lanes):
    def emit(r, c0, acc):
        base = cb_ref[r, pl.ds(c0, 8), lanes].astype(jnp.float32)
        upd = (acc + 8.0 * base) * inv_ref[r, pl.ds(c0, 8), :]
        out_ref[r, pl.ds(c0, 8), lanes] = upd.astype(out_ref.dtype)

    return emit


def inverter(inv_ref):
    def emit(r, c0, acc):
        inv_ref[r, pl.ds(c0, 8), :] = 1.0 / (acc[:, 2:3] + 8.0)

    return emit


def finish_inner(middle, codebook):
    rows, cols, feature = codebook.shape
    lanes = 128
    blocks = feature // lanes

    def kernel(mid_ref, cb_ref, out_ref, inv_ref):
        step = pl.program_id(0)

        def rows_pass(emit):
            def body(i, carry):
                first = RADIUS + i * GROUP

                def read(j, c0, part):
                    return mid_ref[first + j - RADIUS, pl.ds(c0, 8), part]

                row_group(read, first, cols, slice(None), emit)
                return carry

            lax.fori_loop(0, (rows - 2 * RADIUS) // GROUP, body, 0)

        @pl.when(step == 0)
        def _():
            rows_pass(inverter(inv_ref))

        @pl.when(step > 0)
        def _():
            rows_pass(updater(cb_ref, inv_ref, out_ref, slice(None)))

    out_spec = pl.BlockSpec((rows, cols, lanes), lambda j: (0, 0, jnp.maximum(j - 1, 0)))
    return pl.pallas_call(
        kernel,
        grid=(blocks + 1,),
        in_specs=[
            pl.BlockSpec((rows, cols, lanes), lambda j: (0, 0, (j + blocks) % (blocks + 1))),
            out_spec,
        ],
        out_specs=out_spec,
        out_shape=jax.ShapeDtypeStruct(codebook.shape, codebook.dtype),
        scratch_shapes=[pltpu.VMEM((rows, cols, 1), jnp.float32)],
    )(middle, codebook)


def finish_edges(above, middle, below, codebook, partial):
    rows, cols, feature = codebook.shape
    width = middle.shape[2]
    lanes = 128
    near = 2 * RADIUS
    last_edge = rows // RADIUS - 1

    def kernel(above_ref, mid_ref, below_ref, cb_ref, prev_ref, out_ref, ext_ref, inv_ref):
        del prev_ref
        side = pl.program_id(0)

        @pl.when(side == 0)
        def _():
            ext_ref[0:RADIUS] = above_ref[...]
            ext_ref[RADIUS:] = mid_ref[...]

        @pl.when(side == 1)
        def _():
            ext_ref[0:near] = mid_ref[...]
            ext_ref[near:] = below_ref[...]

        def body(i, carry):
            first = i * GROUP

            def read(j, c0, part):
                return ext_ref[first + j, pl.ds(c0, 8), part]

            row_group(read, first, cols, pl.ds(feature, lanes), inverter(inv_ref))
            for lane in range(0, feature, lanes):
                part = pl.ds(lane, lanes)
                row_group(read, first, cols, part, updater(cb_ref, inv_ref, out_ref, part))
            return carry

        lax.fori_loop(0, RADIUS // GROUP, body, 0)

    halo_spec = pl.BlockSpec((RADIUS, cols, width), lambda i: (0, 0, 0))
    edge_spec = pl.BlockSpec((RADIUS, cols, feature), lambda i: (i * last_edge, 0, 0))
    return pl.pallas_call(
        kernel,
        grid=(2,),
        in_specs=[
            halo_spec,
            pl.BlockSpec((near, cols, width), lambda i: (i * (rows // near - 1), 0, 0)),
            halo_spec,
            edge_spec,
            pl.BlockSpec(memory_space=pl.ANY),
        ],
        out_specs=edge_spec,
        out_shape=jax.ShapeDtypeStruct(codebook.shape, codebook.dtype),
        scratch_shapes=[
            pltpu.VMEM((near + RADIUS, cols, width), jnp.float32),
            pltpu.VMEM((RADIUS, cols, 1), jnp.float32),
        ],
        input_output_aliases={4: 0},
    )(above, middle, below, codebook, partial)


def exchange(lead, last, axis):
    devices = lax.axis_size(axis)
    up = [(i, i + 1) for i in range(devices - 1)]
    down = [(j, i) for i, j in up]
    return lax.ppermute(last, axis, up), lax.ppermute(lead, axis, down)


def on_device(documents, owner_tile, unit_in_tile, codebook):
    rows_mx = lax.axis_size("mx")
    cols_my = lax.axis_size("my")
    tile_total = rows_mx * cols_my
    rows_tile, cols_tile, feature = codebook.shape
    doc_count = documents.shape[0]
    capacity = max(2, 2 * doc_count // tile_total)
    target = owner_tile[:, 0]
    tile_hits = (target[:, None] == jnp.arange(tile_total, dtype=jnp.int32)[None, :]).astype(
        jnp.int32
    )
    earlier = jnp.cumsum(tile_hits, axis=0) - tile_hits
    slot_pos = jnp.sum(earlier * tile_hits, axis=1)
    unit_row = unit_in_tile // cols_tile
    unit_col = unit_in_tile % cols_tile
    extra = jnp.zeros((doc_count, 128), jnp.bfloat16)
    extra = extra.at[:, 0].set(unit_row.astype(jnp.bfloat16))
    extra = extra.at[:, 1].set(unit_col.astype(jnp.bfloat16))
    extra = extra.at[:, 2].set(1.0)
    rows_out = jnp.concatenate([documents, extra], axis=1)
    width = feature + 128
    send_place = target * capacity + slot_pos
    outgoing = jnp.zeros((tile_total * capacity, width), jnp.bfloat16).at[send_place].set(rows_out)
    got = lax.all_to_all(
        outgoing.reshape(tile_total, capacity, width),
        ("mx", "my"),
        split_axis=0,
        concat_axis=0,
        tiled=True,
    ).reshape(-1, width)
    mark_row = got[:, feature].astype(jnp.int32)
    mark_col = got[:, feature + 1].astype(jnp.int32)
    unit_ids = jnp.where(got[:, feature + 2] > 0.5, mark_row * cols_tile + mark_col, -1)
    col_total = cols_tile // RADIUS
    bands = accumulate(unit_ids, got, rows_tile, cols_tile, feature, [0, col_total - 1])
    last = cols_tile - RADIUS
    bands, lead, tail = bands
    from_left, from_right = exchange(lead, tail, "my")
    inner = list(range(1, col_total - 1))
    (numerator,) = accumulate(unit_ids, got, rows_tile, cols_tile, feature, inner, bands)

    g_rows = jnp.asarray(band_matrix(rows_tile))
    g_cols = jnp.asarray(band_matrix(cols_tile))
    last = rows_tile - RADIUS

    def col_pass(lo, hi):
        pieces = [from_left[lo:hi], numerator[lo:hi], from_right[lo:hi]]
        return jnp.einsum("ck,rke->rce", g_cols, jnp.concatenate(pieces, axis=1), precision=HI)

    col_top, col_bottom = col_pass(0, RADIUS), col_pass(last, rows_tile)

    above, below = exchange(col_top, col_bottom, "mx")
    col_num = col_pass(0, rows_tile)
    partial = finish_inner(col_num, codebook)
    return finish_edges(above, col_num, below, codebook, partial)


def solution(mesh):
    return jax.shard_map(
        on_device,
        mesh=mesh,
        in_specs=(
            P(("mx", "my"), None),
            P(("mx", "my"), None),
            P(("mx", "my")),
            P("mx", "my", None),
        ),
        out_specs=P("mx", "my", None),
        check_vma=False,
    )
```

```python
import math

import jax
import jax.numpy as jnp
import numpy as np
from jax import lax
from jax.experimental import pallas as pl
from jax.experimental.pallas import tpu as pltpu
from jax.sharding import PartitionSpec as P

RADIUS = 8
HI = lax.Precision.HIGH


def band_matrix(out_len):
    ext = out_len + 2 * RADIUS
    mat = np.zeros((out_len, ext), np.float32)
    for r in range(out_len):
        for k in range(-RADIUS, RADIUS + 1):
            mat[r, r + k + RADIUS] = math.exp(-2.0 * k * k / RADIUS**2)
    return mat


def accumulate(ids, docs, rows_tile, cols_tile, feature, col_blocks, prior=None):
    rows, width = docs.shape
    band = rows_tile * RADIUS
    picks = jnp.asarray(col_blocks, jnp.int32)

    def kernel(picks_ref, ids_ref, docs_ref, *refs):
        num_ref = refs[-1] if prior is not None else refs[-3]
        place = lax.broadcasted_iota(jnp.int32, (band, rows), 0)
        first_col = picks_ref[pl.program_id(0)] * RADIUS
        units = (place // RADIUS) * cols_tile + first_col + place % RADIUS
        one_hot = (units == ids_ref[...]).astype(jnp.bfloat16)
        sums = jnp.dot(one_hot, docs_ref[...], preferred_element_type=jnp.float32)
        num_ref[...] = sums.reshape(rows_tile, RADIUS, width)
        if prior is None:
            for side in range(2):

                @pl.when(pl.program_id(0) == side)
                def _():
                    refs[side - 2][...] = sums.reshape(rows_tile, RADIUS, width)

    out_specs = [pl.BlockSpec((rows_tile, RADIUS, width), lambda j, p: (0, p[j], 0))]
    out_shape = [jax.ShapeDtypeStruct((rows_tile, cols_tile, width), jnp.float32)]
    if prior is None:
        out_specs += [pl.BlockSpec((rows_tile, RADIUS, width), lambda j, p: (0, 0, 0))] * 2
        out_shape += [jax.ShapeDtypeStruct((rows_tile, RADIUS, width), jnp.float32)] * 2
    in_specs = [
        pl.BlockSpec((1, rows), lambda j, p: (0, 0)),
        pl.BlockSpec((rows, width), lambda j, p: (0, 0)),
    ]
    operands = [ids.reshape(1, rows), docs]
    aliases = {}
    if prior is not None:
        in_specs += [pl.BlockSpec(memory_space=pl.ANY)]
        operands += [prior]
        aliases = {3: 0}
    return pl.pallas_call(
        kernel,
        grid_spec=pltpu.PrefetchScalarGridSpec(
            num_scalar_prefetch=1,
            grid=(len(col_blocks),),
            in_specs=in_specs,
            out_specs=out_specs,
        ),
        out_shape=out_shape,
        input_output_aliases=aliases,
    )(picks, *operands)


TAPS = [math.exp(-2.0 * k * k / RADIUS**2) for k in range(RADIUS + 1)]
GROUP = 4


def row_group(read, first, cols, lanes, emit):
    for c0 in range(0, cols, 8):
        window = [read(j, c0, lanes) for j in range(GROUP + 2 * RADIUS)]
        for q in range(GROUP):
            centre = q + RADIUS
            acc = TAPS[0] * window[centre]
            for k in range(1, RADIUS + 1):
                acc = acc + TAPS[k] * (window[centre - k] + window[centre + k])
            emit(first + q, c0, acc)


def updater(cb_ref, inv_ref, out_ref, lanes):
    def emit(r, c0, acc):
        base = cb_ref[r, pl.ds(c0, 8), lanes].astype(jnp.float32)
        upd = (acc + 8.0 * base) * inv_ref[r, pl.ds(c0, 8), :]
        out_ref[r, pl.ds(c0, 8), lanes] = upd.astype(out_ref.dtype)

    return emit


def inverter(inv_ref):
    def emit(r, c0, acc):
        inv_ref[r, pl.ds(c0, 8), :] = 1.0 / (acc[:, 2:3] + 8.0)

    return emit


def piece_reader(refs, row_of):
    left_ref, inner_ref, right_ref = refs
    span = inner_ref.shape[1]

    def read(j, c0, part):
        row = row_of(j)
        if c0 < RADIUS:
            return left_ref[row, pl.ds(c0, 8), part]
        if c0 < RADIUS + span:
            return inner_ref[row, pl.ds(c0 - RADIUS, 8), part]
        return right_ref[row, pl.ds(c0 - RADIUS - span, 8), part]

    return read


def finish_inner(pieces, codebook):
    rows, cols, feature = codebook.shape
    lanes = 128
    blocks = feature // lanes

    def kernel(left_ref, inner_ref, right_ref, cb_ref, out_ref, inv_ref):
        step = pl.program_id(0)

        def rows_pass(emit):
            def body(i, carry):
                first = RADIUS + i * GROUP
                read = piece_reader((left_ref, inner_ref, right_ref), lambda j: first + j - RADIUS)
                row_group(read, first, cols, slice(None), emit)
                return carry

            lax.fori_loop(0, (rows - 2 * RADIUS) // GROUP, body, 0)

        @pl.when(step == 0)
        def _():
            rows_pass(inverter(inv_ref))

        @pl.when(step > 0)
        def _():
            rows_pass(updater(cb_ref, inv_ref, out_ref, slice(None)))

    def piece_spec(piece):
        return pl.BlockSpec((rows, piece.shape[1], lanes), lambda j: (0, 0, (j + blocks) % (blocks + 1)))

    out_spec = pl.BlockSpec((rows, cols, lanes), lambda j: (0, 0, jnp.maximum(j - 1, 0)))
    return pl.pallas_call(
        kernel,
        grid=(blocks + 1,),
        in_specs=[piece_spec(p) for p in pieces] + [out_spec],
        out_specs=out_spec,
        out_shape=jax.ShapeDtypeStruct(codebook.shape, codebook.dtype),
        scratch_shapes=[pltpu.VMEM((rows, cols, 1), jnp.float32)],
    )(*pieces, codebook)


def finish_edges(above, pieces, below, codebook, partial):
    rows, cols, feature = codebook.shape
    width = above.shape[2]
    lanes = 128
    near = 2 * RADIUS
    last_edge = rows // RADIUS - 1
    span = pieces[1].shape[1]

    def kernel(above_ref, left_ref, inner_ref, right_ref, below_ref, cb_ref, prev_ref, out_ref, ext_ref, inv_ref):
        del prev_ref
        side = pl.program_id(0)

        def fill(lo):
            ext_ref[lo : lo + near, 0:RADIUS] = left_ref[...]
            ext_ref[lo : lo + near, RADIUS : RADIUS + span] = inner_ref[...]
            ext_ref[lo : lo + near, RADIUS + span :] = right_ref[...]

        @pl.when(side == 0)
        def _():
            ext_ref[0:RADIUS] = above_ref[...]
            fill(RADIUS)

        @pl.when(side == 1)
        def _():
            fill(0)
            ext_ref[near:] = below_ref[...]

        def body(i, carry):
            first = i * GROUP

            def read(j, c0, part):
                return ext_ref[first + j, pl.ds(c0, 8), part]

            row_group(read, first, cols, pl.ds(feature, lanes), inverter(inv_ref))
            for lane in range(0, feature, lanes):
                part = pl.ds(lane, lanes)
                row_group(read, first, cols, part, updater(cb_ref, inv_ref, out_ref, part))
            return carry

        lax.fori_loop(0, RADIUS // GROUP, body, 0)

    halo_spec = pl.BlockSpec((RADIUS, cols, width), lambda i: (0, 0, 0))
    edge_spec = pl.BlockSpec((RADIUS, cols, feature), lambda i: (i * last_edge, 0, 0))

    def piece_spec(piece):
        return pl.BlockSpec((near, piece.shape[1], width), lambda i: (i * (rows // near - 1), 0, 0))

    return pl.pallas_call(
        kernel,
        grid=(2,),
        in_specs=[halo_spec] + [piece_spec(p) for p in pieces] + [
            halo_spec,
            edge_spec,
            pl.BlockSpec(memory_space=pl.ANY),
        ],
        out_specs=edge_spec,
        out_shape=jax.ShapeDtypeStruct(codebook.shape, codebook.dtype),
        scratch_shapes=[
            pltpu.VMEM((near + RADIUS, cols, width), jnp.float32),
            pltpu.VMEM((RADIUS, cols, 1), jnp.float32),
        ],
        input_output_aliases={6: 0},
    )(above, *pieces, below, codebook, partial)


def exchange(lead, last, axis):
    devices = lax.axis_size(axis)
    up = [(i, i + 1) for i in range(devices - 1)]
    down = [(j, i) for i, j in up]
    return lax.ppermute(last, axis, up), lax.ppermute(lead, axis, down)


def on_device(documents, owner_tile, unit_in_tile, codebook):
    rows_mx = lax.axis_size("mx")
    cols_my = lax.axis_size("my")
    tile_total = rows_mx * cols_my
    rows_tile, cols_tile, feature = codebook.shape
    doc_count = documents.shape[0]
    capacity = max(2, 2 * doc_count // tile_total)
    target = owner_tile[:, 0]
    tile_hits = (target[:, None] == jnp.arange(tile_total, dtype=jnp.int32)[None, :]).astype(
        jnp.int32
    )
    earlier = jnp.cumsum(tile_hits, axis=0) - tile_hits
    slot_pos = jnp.sum(earlier * tile_hits, axis=1)
    unit_row = unit_in_tile // cols_tile
    unit_col = unit_in_tile % cols_tile
    extra = jnp.zeros((doc_count, 128), jnp.bfloat16)
    extra = extra.at[:, 0].set(unit_row.astype(jnp.bfloat16))
    extra = extra.at[:, 1].set(unit_col.astype(jnp.bfloat16))
    extra = extra.at[:, 2].set(1.0)
    rows_out = jnp.concatenate([documents, extra], axis=1)
    width = feature + 128
    send_place = target * capacity + slot_pos
    outgoing = jnp.zeros((tile_total * capacity, width), jnp.bfloat16).at[send_place].set(rows_out)
    got = lax.all_to_all(
        outgoing.reshape(tile_total, capacity, width),
        ("mx", "my"),
        split_axis=0,
        concat_axis=0,
        tiled=True,
    ).reshape(-1, width)
    mark_row = got[:, feature].astype(jnp.int32)
    mark_col = got[:, feature + 1].astype(jnp.int32)
    unit_ids = jnp.where(got[:, feature + 2] > 0.5, mark_row * cols_tile + mark_col, -1)
    col_total = cols_tile // RADIUS
    bands = accumulate(unit_ids, got, rows_tile, cols_tile, feature, [0, col_total - 1])
    last = cols_tile - RADIUS
    bands, lead, tail = bands
    from_left, from_right = exchange(lead, tail, "my")
    inner = list(range(1, col_total - 1))
    (numerator,) = accumulate(unit_ids, got, rows_tile, cols_tile, feature, inner, bands)

    g_cols = jnp.asarray(band_matrix(cols_tile))
    inner_piece = jnp.einsum(
        "ck,rke->rce", g_cols[RADIUS : cols_tile - RADIUS, RADIUS : RADIUS + cols_tile], numerator,
        precision=HI,
    )
    from_left, from_right, inner_piece = lax.optimization_barrier((from_left, from_right, inner_piece))
    last = rows_tile - RADIUS

    def col_pass(lo, hi):
        pieces = [from_left[lo:hi], numerator[lo:hi], from_right[lo:hi]]
        return jnp.einsum("ck,rke->rce", g_cols, jnp.concatenate(pieces, axis=1), precision=HI)

    col_top, col_bottom = col_pass(0, RADIUS), col_pass(last, rows_tile)

    above, below = exchange(col_top, col_bottom, "mx")
    right_start = cols_tile - 2 * RADIUS
    left_piece = jnp.einsum(
        "ck,rke->rce",
        g_cols[:RADIUS, : 3 * RADIUS],
        jnp.concatenate([from_left, numerator[:, : 2 * RADIUS]], axis=1),
        precision=HI,
    )
    right_piece = jnp.einsum(
        "ck,rke->rce",
        g_cols[:RADIUS, : 3 * RADIUS],
        jnp.concatenate([numerator[:, right_start:], from_right], axis=1),
        precision=HI,
    )
    pieces = (left_piece, inner_piece, right_piece)
    partial = finish_inner(pieces, codebook)
    return finish_edges(above, pieces, below, codebook, partial)


def solution(mesh):
    return jax.shard_map(
        on_device,
        mesh=mesh,
        in_specs=(
            P(("mx", "my"), None),
            P(("mx", "my"), None),
            P(("mx", "my")),
            P("mx", "my", None),
        ),
        out_specs=P("mx", "my", None),
        check_vma=False,
    )
```

```python
import math

import jax
import jax.numpy as jnp
import numpy as np
from jax import lax
from jax.experimental import pallas as pl
from jax.experimental.pallas import tpu as pltpu
from jax.sharding import PartitionSpec as P

RADIUS = 8
HI = lax.Precision.HIGH


def band_matrix(out_len):
    ext = out_len + 2 * RADIUS
    mat = np.zeros((out_len, ext), np.float32)
    for r in range(out_len):
        for k in range(-RADIUS, RADIUS + 1):
            mat[r, r + k + RADIUS] = math.exp(-2.0 * k * k / RADIUS**2)
    return mat


def accumulate(ids, docs, rows_tile, cols_tile, feature, col_blocks, prior=None):
    rows, width = docs.shape
    band = rows_tile * RADIUS
    picks = jnp.asarray(col_blocks, jnp.int32)

    def kernel(picks_ref, ids_ref, docs_ref, *refs):
        num_ref = refs[-1] if prior is not None else refs[-3]
        place = lax.broadcasted_iota(jnp.int32, (band, rows), 0)
        first_col = picks_ref[pl.program_id(0)] * RADIUS
        units = (place // RADIUS) * cols_tile + first_col + place % RADIUS
        one_hot = (units == ids_ref[...]).astype(jnp.bfloat16)
        sums = jnp.dot(one_hot, docs_ref[...], preferred_element_type=jnp.float32)
        num_ref[...] = sums.reshape(rows_tile, RADIUS, width)
        if prior is None:
            for side in range(2):

                @pl.when(pl.program_id(0) == side)
                def _():
                    refs[side - 2][...] = sums.reshape(rows_tile, RADIUS, width)

    out_specs = [pl.BlockSpec((rows_tile, RADIUS, width), lambda j, p: (0, p[j], 0))]
    out_shape = [jax.ShapeDtypeStruct((rows_tile, cols_tile, width), jnp.float32)]
    if prior is None:
        out_specs += [pl.BlockSpec((rows_tile, RADIUS, width), lambda j, p: (0, 0, 0))] * 2
        out_shape += [jax.ShapeDtypeStruct((rows_tile, RADIUS, width), jnp.float32)] * 2
    in_specs = [
        pl.BlockSpec((1, rows), lambda j, p: (0, 0)),
        pl.BlockSpec((rows, width), lambda j, p: (0, 0)),
    ]
    operands = [ids.reshape(1, rows), docs]
    aliases = {}
    if prior is not None:
        in_specs += [pl.BlockSpec(memory_space=pl.ANY)]
        operands += [prior]
        aliases = {3: 0}
    return pl.pallas_call(
        kernel,
        grid_spec=pltpu.PrefetchScalarGridSpec(
            num_scalar_prefetch=1,
            grid=(len(col_blocks),),
            in_specs=in_specs,
            out_specs=out_specs,
        ),
        out_shape=out_shape,
        input_output_aliases=aliases,
    )(picks, *operands)


TAPS = [math.exp(-2.0 * k * k / RADIUS**2) for k in range(RADIUS + 1)]
GROUP = 8


def row_group(read, first, cols, lanes, emit):
    for c0 in range(0, cols, 8):
        window = [read(j, c0, lanes) for j in range(GROUP + 2 * RADIUS)]
        for q in range(GROUP):
            centre = q + RADIUS
            acc = TAPS[0] * window[centre]
            for k in range(1, RADIUS + 1):
                acc = acc + TAPS[k] * (window[centre - k] + window[centre + k])
            emit(first + q, c0, acc)


def updater(cb_ref, inv_ref, out_ref, lanes):
    def emit(r, c0, acc):
        base = cb_ref[r, pl.ds(c0, 8), lanes].astype(jnp.float32)
        upd = (acc + 8.0 * base) * inv_ref[r, pl.ds(c0, 8), :]
        out_ref[r, pl.ds(c0, 8), lanes] = upd.astype(out_ref.dtype)

    return emit


def inverter(inv_ref):
    def emit(r, c0, acc):
        inv_ref[r, pl.ds(c0, 8), :] = 1.0 / (acc[:, 2:3] + 8.0)

    return emit


def finish_inner(middle, codebook):
    rows, cols, feature = codebook.shape
    lanes = 128
    blocks = feature // lanes

    def kernel(mid_ref, cb_ref, out_ref, inv_ref):
        step = pl.program_id(0)

        def rows_pass(emit):
            def body(i, carry):
                first = RADIUS + i * GROUP

                def read(j, c0, part):
                    return mid_ref[first + j - RADIUS, pl.ds(c0, 8), part]

                row_group(read, first, cols, slice(None), emit)
                return carry

            lax.fori_loop(0, (rows - 2 * RADIUS) // GROUP, body, 0)

        @pl.when(step == 0)
        def _():
            rows_pass(inverter(inv_ref))

        @pl.when(step > 0)
        def _():
            rows_pass(updater(cb_ref, inv_ref, out_ref, slice(None)))

    out_spec = pl.BlockSpec((rows, cols, lanes), lambda j: (0, 0, jnp.maximum(j - 1, 0)))
    return pl.pallas_call(
        kernel,
        grid=(blocks + 1,),
        in_specs=[
            pl.BlockSpec((rows, cols, lanes), lambda j: (0, 0, (j + blocks) % (blocks + 1))),
            out_spec,
        ],
        out_specs=out_spec,
        out_shape=jax.ShapeDtypeStruct(codebook.shape, codebook.dtype),
        scratch_shapes=[pltpu.VMEM((rows, cols, 1), jnp.float32)],
    )(middle, codebook)


def finish_edges(above, middle, below, codebook, partial):
    rows, cols, feature = codebook.shape
    width = middle.shape[2]
    lanes = 128
    near = 2 * RADIUS
    last_edge = rows // RADIUS - 1

    def kernel(above_ref, mid_ref, below_ref, cb_ref, prev_ref, out_ref, ext_ref, inv_ref):
        del prev_ref
        side = pl.program_id(0)

        @pl.when(side == 0)
        def _():
            ext_ref[0:RADIUS] = above_ref[...]
            ext_ref[RADIUS:] = mid_ref[...]

        @pl.when(side == 1)
        def _():
            ext_ref[0:near] = mid_ref[...]
            ext_ref[near:] = below_ref[...]

        def body(i, carry):
            first = i * GROUP

            def read(j, c0, part):
                return ext_ref[first + j, pl.ds(c0, 8), part]

            row_group(read, first, cols, pl.ds(feature, lanes), inverter(inv_ref))
            for lane in range(0, feature, lanes):
                part = pl.ds(lane, lanes)
                row_group(read, first, cols, part, updater(cb_ref, inv_ref, out_ref, part))
            return carry

        lax.fori_loop(0, RADIUS // GROUP, body, 0)

    halo_spec = pl.BlockSpec((RADIUS, cols, width), lambda i: (0, 0, 0))
    edge_spec = pl.BlockSpec((RADIUS, cols, feature), lambda i: (i * last_edge, 0, 0))
    return pl.pallas_call(
        kernel,
        grid=(2,),
        in_specs=[
            halo_spec,
            pl.BlockSpec((near, cols, width), lambda i: (i * (rows // near - 1), 0, 0)),
            halo_spec,
            edge_spec,
            pl.BlockSpec(memory_space=pl.ANY),
        ],
        out_specs=edge_spec,
        out_shape=jax.ShapeDtypeStruct(codebook.shape, codebook.dtype),
        scratch_shapes=[
            pltpu.VMEM((near + RADIUS, cols, width), jnp.float32),
            pltpu.VMEM((RADIUS, cols, 1), jnp.float32),
        ],
        input_output_aliases={4: 0},
    )(above, middle, below, codebook, partial)


def exchange(lead, last, axis):
    devices = lax.axis_size(axis)
    up = [(i, i + 1) for i in range(devices - 1)]
    down = [(j, i) for i, j in up]
    return lax.ppermute(last, axis, up), lax.ppermute(lead, axis, down)


def on_device(documents, owner_tile, unit_in_tile, codebook):
    rows_mx = lax.axis_size("mx")
    cols_my = lax.axis_size("my")
    tile_total = rows_mx * cols_my
    rows_tile, cols_tile, feature = codebook.shape
    doc_count = documents.shape[0]
    capacity = max(2, 2 * doc_count // tile_total)
    target = owner_tile[:, 0]
    tile_hits = (target[:, None] == jnp.arange(tile_total, dtype=jnp.int32)[None, :]).astype(
        jnp.int32
    )
    earlier = jnp.cumsum(tile_hits, axis=0) - tile_hits
    slot_pos = jnp.sum(earlier * tile_hits, axis=1)
    unit_row = unit_in_tile // cols_tile
    unit_col = unit_in_tile % cols_tile
    extra = jnp.zeros((doc_count, 128), jnp.bfloat16)
    extra = extra.at[:, 0].set(unit_row.astype(jnp.bfloat16))
    extra = extra.at[:, 1].set(unit_col.astype(jnp.bfloat16))
    extra = extra.at[:, 2].set(1.0)
    rows_out = jnp.concatenate([documents, extra], axis=1)
    width = feature + 128
    send_place = target * capacity + slot_pos
    outgoing = jnp.zeros((tile_total * capacity, width), jnp.bfloat16).at[send_place].set(rows_out)
    got = lax.all_to_all(
        outgoing.reshape(tile_total, capacity, width),
        ("mx", "my"),
        split_axis=0,
        concat_axis=0,
        tiled=True,
    ).reshape(-1, width)
    mark_row = got[:, feature].astype(jnp.int32)
    mark_col = got[:, feature + 1].astype(jnp.int32)
    unit_ids = jnp.where(got[:, feature + 2] > 0.5, mark_row * cols_tile + mark_col, -1)
    col_total = cols_tile // RADIUS
    bands = accumulate(unit_ids, got, rows_tile, cols_tile, feature, [0, col_total - 1])
    last = cols_tile - RADIUS
    bands, lead, tail = bands
    from_left, from_right = exchange(lead, tail, "my")
    inner = list(range(1, col_total - 1))
    (numerator,) = accumulate(unit_ids, got, rows_tile, cols_tile, feature, inner, bands)

    g_rows = jnp.asarray(band_matrix(rows_tile))
    g_cols = jnp.asarray(band_matrix(cols_tile))
    last = rows_tile - RADIUS

    def col_pass(lo, hi):
        pieces = [from_left[lo:hi], numerator[lo:hi], from_right[lo:hi]]
        return jnp.einsum("ck,rke->rce", g_cols, jnp.concatenate(pieces, axis=1), precision=HI)

    col_top, col_bottom = col_pass(0, RADIUS), col_pass(last, rows_tile)

    above, below = exchange(col_top, col_bottom, "mx")
    col_num = col_pass(0, rows_tile)
    partial = finish_inner(col_num, codebook)
    return finish_edges(above, col_num, below, codebook, partial)


def solution(mesh):
    return jax.shard_map(
        on_device,
        mesh=mesh,
        in_specs=(
            P(("mx", "my"), None),
            P(("mx", "my"), None),
            P(("mx", "my")),
            P("mx", "my", None),
        ),
        out_specs=P("mx", "my", None),
        check_vma=False,
    )
```

```python
import math

import jax
import jax.numpy as jnp
import numpy as np
from jax import lax
from jax.experimental import pallas as pl
from jax.experimental.pallas import tpu as pltpu
from jax.sharding import PartitionSpec as P

RADIUS = 8
HI = lax.Precision.HIGH


def band_matrix(out_len):
    ext = out_len + 2 * RADIUS
    mat = np.zeros((out_len, ext), np.float32)
    for r in range(out_len):
        for k in range(-RADIUS, RADIUS + 1):
            mat[r, r + k + RADIUS] = math.exp(-2.0 * k * k / RADIUS**2)
    return mat


def accumulate_bands(ids, docs, rows_tile, cols_tile):
    rows, width = docs.shape
    band = rows_tile * RADIUS

    def kernel(ids_ref, docs_ref, lead_ref, tail_ref):
        place = lax.broadcasted_iota(jnp.int32, (2 * band, rows), 0)
        side = place // band
        within = place % band
        units = (within // RADIUS) * cols_tile + side * (cols_tile - RADIUS) + within % RADIUS
        one_hot = (units == ids_ref[...]).astype(jnp.bfloat16)
        sums = jnp.dot(one_hot, docs_ref[...], preferred_element_type=jnp.float32)
        lead_ref[...] = sums[:band].reshape(rows_tile, RADIUS, width)
        tail_ref[...] = sums[band:].reshape(rows_tile, RADIUS, width)

    band_shape = jax.ShapeDtypeStruct((rows_tile, RADIUS, width), jnp.float32)
    return pl.pallas_call(kernel, out_shape=[band_shape, band_shape])(ids.reshape(1, rows), docs)


def accumulate(ids, docs, rows_tile, cols_tile, lead, tail):
    rows, width = docs.shape
    band = rows_tile * RADIUS
    blocks = cols_tile // RADIUS

    def kernel(ids_ref, docs_ref, lead_ref, tail_ref, num_ref):
        step = pl.program_id(0)

        @pl.when(step == 0)
        def _():
            num_ref[...] = lead_ref[...]

        @pl.when(step == blocks - 1)
        def _():
            num_ref[...] = tail_ref[...]

        @pl.when((step > 0) & (step < blocks - 1))
        def _():
            place = lax.broadcasted_iota(jnp.int32, (band, rows), 0)
            units = (place // RADIUS) * cols_tile + step * RADIUS + place % RADIUS
            one_hot = (units == ids_ref[...]).astype(jnp.bfloat16)
            sums = jnp.dot(one_hot, docs_ref[...], preferred_element_type=jnp.float32)
            num_ref[...] = sums.reshape(rows_tile, RADIUS, width)

    band_spec = pl.BlockSpec((rows_tile, RADIUS, width), lambda j: (0, 0, 0))
    return pl.pallas_call(
        kernel,
        grid=(blocks,),
        in_specs=[
            pl.BlockSpec((1, rows), lambda j: (0, 0)),
            pl.BlockSpec((rows, width), lambda j: (0, 0)),
            band_spec,
            band_spec,
        ],
        out_specs=pl.BlockSpec((rows_tile, RADIUS, width), lambda j: (0, j, 0)),
        out_shape=jax.ShapeDtypeStruct((rows_tile, cols_tile, width), jnp.float32),
    )(ids.reshape(1, rows), docs, lead, tail)


TAPS = [math.exp(-2.0 * k * k / RADIUS**2) for k in range(RADIUS + 1)]
GROUP = 4


def row_group(read, first, cols, lanes, emit):
    for c0 in range(0, cols, 8):
        window = [read(j, c0, lanes) for j in range(GROUP + 2 * RADIUS)]
        for q in range(GROUP):
            centre = q + RADIUS
            acc = TAPS[0] * window[centre]
            for k in range(1, RADIUS + 1):
                acc = acc + TAPS[k] * (window[centre - k] + window[centre + k])
            emit(first + q, c0, acc)


def updater(cb_ref, inv_ref, out_ref, lanes):
    def emit(r, c0, acc):
        base = cb_ref[r, pl.ds(c0, 8), lanes].astype(jnp.float32)
        upd = (acc + 8.0 * base) * inv_ref[r, pl.ds(c0, 8), :]
        out_ref[r, pl.ds(c0, 8), lanes] = upd.astype(out_ref.dtype)

    return emit


def inverter(inv_ref):
    def emit(r, c0, acc):
        inv_ref[r, pl.ds(c0, 8), :] = 1.0 / (acc[:, 2:3] + 8.0)

    return emit


def finish_inner(middle, codebook):
    rows, cols, feature = codebook.shape
    lanes = 128
    blocks = feature // lanes

    def kernel(mid_ref, cb_ref, out_ref, inv_ref):
        step = pl.program_id(0)

        def rows_pass(emit):
            def body(i, carry):
                first = RADIUS + i * GROUP

                def read(j, c0, part):
                    return mid_ref[first + j - RADIUS, pl.ds(c0, 8), part]

                row_group(read, first, cols, slice(None), emit)
                return carry

            lax.fori_loop(0, (rows - 2 * RADIUS) // GROUP, body, 0)

        @pl.when(step == 0)
        def _():
            rows_pass(inverter(inv_ref))

        @pl.when(step > 0)
        def _():
            rows_pass(updater(cb_ref, inv_ref, out_ref, slice(None)))

    out_spec = pl.BlockSpec((rows, cols, lanes), lambda j: (0, 0, jnp.maximum(j - 1, 0)))
    return pl.pallas_call(
        kernel,
        grid=(blocks + 1,),
        in_specs=[
            pl.BlockSpec((rows, cols, lanes), lambda j: (0, 0, (j + blocks) % (blocks + 1))),
            out_spec,
        ],
        out_specs=out_spec,
        out_shape=jax.ShapeDtypeStruct(codebook.shape, codebook.dtype),
        scratch_shapes=[pltpu.VMEM((rows, cols, 1), jnp.float32)],
    )(middle, codebook)


def finish_edges(above, middle, below, codebook, partial):
    rows, cols, feature = codebook.shape
    width = middle.shape[2]
    lanes = 128
    near = 2 * RADIUS
    last_edge = rows // RADIUS - 1

    def kernel(above_ref, mid_ref, below_ref, cb_ref, prev_ref, out_ref, ext_ref, inv_ref):
        del prev_ref
        side = pl.program_id(0)

        @pl.when(side == 0)
        def _():
            ext_ref[0:RADIUS] = above_ref[...]
            ext_ref[RADIUS:] = mid_ref[...]

        @pl.when(side == 1)
        def _():
            ext_ref[0:near] = mid_ref[...]
            ext_ref[near:] = below_ref[...]

        def body(i, carry):
            first = i * GROUP

            def read(j, c0, part):
                return ext_ref[first + j, pl.ds(c0, 8), part]

            row_group(read, first, cols, pl.ds(feature, lanes), inverter(inv_ref))
            for lane in range(0, feature, lanes):
                part = pl.ds(lane, lanes)
                row_group(read, first, cols, part, updater(cb_ref, inv_ref, out_ref, part))
            return carry

        lax.fori_loop(0, RADIUS // GROUP, body, 0)

    halo_spec = pl.BlockSpec((RADIUS, cols, width), lambda i: (0, 0, 0))
    edge_spec = pl.BlockSpec((RADIUS, cols, feature), lambda i: (i * last_edge, 0, 0))
    return pl.pallas_call(
        kernel,
        grid=(2,),
        in_specs=[
            halo_spec,
            pl.BlockSpec((near, cols, width), lambda i: (i * (rows // near - 1), 0, 0)),
            halo_spec,
            edge_spec,
            pl.BlockSpec(memory_space=pl.ANY),
        ],
        out_specs=edge_spec,
        out_shape=jax.ShapeDtypeStruct(codebook.shape, codebook.dtype),
        scratch_shapes=[
            pltpu.VMEM((near + RADIUS, cols, width), jnp.float32),
            pltpu.VMEM((RADIUS, cols, 1), jnp.float32),
        ],
        input_output_aliases={4: 0},
    )(above, middle, below, codebook, partial)


def exchange(lead, last, axis):
    devices = lax.axis_size(axis)
    up = [(i, i + 1) for i in range(devices - 1)]
    down = [(j, i) for i, j in up]
    return lax.ppermute(last, axis, up), lax.ppermute(lead, axis, down)


def on_device(documents, owner_tile, unit_in_tile, codebook):
    rows_mx = lax.axis_size("mx")
    cols_my = lax.axis_size("my")
    tile_total = rows_mx * cols_my
    rows_tile, cols_tile, feature = codebook.shape
    doc_count = documents.shape[0]
    capacity = max(2, 2 * doc_count // tile_total)
    target = owner_tile[:, 0]
    tile_hits = (target[:, None] == jnp.arange(tile_total, dtype=jnp.int32)[None, :]).astype(
        jnp.int32
    )
    earlier = jnp.cumsum(tile_hits, axis=0) - tile_hits
    slot_pos = jnp.sum(earlier * tile_hits, axis=1)
    unit_row = unit_in_tile // cols_tile
    unit_col = unit_in_tile % cols_tile
    extra = jnp.zeros((doc_count, 128), jnp.bfloat16)
    extra = extra.at[:, 0].set(unit_row.astype(jnp.bfloat16))
    extra = extra.at[:, 1].set(unit_col.astype(jnp.bfloat16))
    extra = extra.at[:, 2].set(1.0)
    rows_out = jnp.concatenate([documents, extra], axis=1)
    width = feature + 128
    send_place = target * capacity + slot_pos
    outgoing = jnp.zeros((tile_total * capacity, width), jnp.bfloat16).at[send_place].set(rows_out)
    got = lax.all_to_all(
        outgoing.reshape(tile_total, capacity, width),
        ("mx", "my"),
        split_axis=0,
        concat_axis=0,
        tiled=True,
    ).reshape(-1, width)
    mark_row = got[:, feature].astype(jnp.int32)
    mark_col = got[:, feature + 1].astype(jnp.int32)
    unit_ids = jnp.where(got[:, feature + 2] > 0.5, mark_row * cols_tile + mark_col, -1)
    col_total = cols_tile // RADIUS
    last = cols_tile - RADIUS
    lead, tail = accumulate_bands(unit_ids, got, rows_tile, cols_tile)
    from_left, from_right = exchange(lead, tail, "my")
    numerator = accumulate(unit_ids, got, rows_tile, cols_tile, lead, tail)

    g_rows = jnp.asarray(band_matrix(rows_tile))
    g_cols = jnp.asarray(band_matrix(cols_tile))
    last = rows_tile - RADIUS

    def col_pass(lo, hi):
        pieces = [from_left[lo:hi], numerator[lo:hi], from_right[lo:hi]]
        return jnp.einsum("ck,rke->rce", g_cols, jnp.concatenate(pieces, axis=1), precision=HI)

    col_top, col_bottom = col_pass(0, RADIUS), col_pass(last, rows_tile)

    above, below = exchange(col_top, col_bottom, "mx")
    col_num = col_pass(0, rows_tile)
    partial = finish_inner(col_num, codebook)
    return finish_edges(above, col_num, below, codebook, partial)


def solution(mesh):
    return jax.shard_map(
        on_device,
        mesh=mesh,
        in_specs=(
            P(("mx", "my"), None),
            P(("mx", "my"), None),
            P(("mx", "my")),
            P("mx", "my", None),
        ),
        out_specs=P("mx", "my", None),
        check_vma=False,
    )
```

```python
import math

import jax
import jax.numpy as jnp
import numpy as np
from jax import lax
from jax.experimental import pallas as pl
from jax.experimental.pallas import tpu as pltpu
from jax.sharding import PartitionSpec as P

RADIUS = 8
HI = lax.Precision.HIGH


def band_matrix(out_len):
    ext = out_len + 2 * RADIUS
    mat = np.zeros((out_len, ext), np.float32)
    for r in range(out_len):
        for k in range(-RADIUS, RADIUS + 1):
            mat[r, r + k + RADIUS] = math.exp(-2.0 * k * k / RADIUS**2)
    return mat


def accumulate_bands(ids, docs, rows_tile, cols_tile):
    rows, width = docs.shape
    band = rows_tile * RADIUS

    def kernel(ids_ref, docs_ref, lead_ref, tail_ref):
        place = lax.broadcasted_iota(jnp.int32, (2 * band, rows), 0)
        side = place // band
        within = place % band
        units = (within // RADIUS) * cols_tile + side * (cols_tile - RADIUS) + within % RADIUS
        one_hot = (units == ids_ref[...]).astype(jnp.bfloat16)
        sums = jnp.dot(one_hot, docs_ref[...], preferred_element_type=jnp.float32)
        lead_ref[...] = sums[:band].reshape(rows_tile, RADIUS, width)
        tail_ref[...] = sums[band:].reshape(rows_tile, RADIUS, width)

    band_shape = jax.ShapeDtypeStruct((rows_tile, RADIUS, width), jnp.float32)
    return pl.pallas_call(kernel, out_shape=[band_shape, band_shape])(ids.reshape(1, rows), docs)


def accumulate(ids, docs, rows_tile, cols_tile, lead, tail):
    rows, width = docs.shape
    span = 2 * RADIUS
    blocks = cols_tile // span

    def kernel(ids_ref, docs_ref, lead_ref, tail_ref, num_ref):
        step = pl.program_id(0)

        def sums_for(first_col, count):
            place = lax.broadcasted_iota(jnp.int32, (rows_tile * count, rows), 0)
            units = (place // count) * cols_tile + first_col + place % count
            one_hot = (units == ids_ref[...]).astype(jnp.bfloat16)
            sums = jnp.dot(one_hot, docs_ref[...], preferred_element_type=jnp.float32)
            return sums.reshape(rows_tile, count, width)

        @pl.when(step == 0)
        def _():
            num_ref[:, :RADIUS] = lead_ref[...]
            num_ref[:, RADIUS:] = sums_for(RADIUS, RADIUS)

        @pl.when(step == blocks - 1)
        def _():
            num_ref[:, :RADIUS] = sums_for(cols_tile - span, RADIUS)
            num_ref[:, RADIUS:] = tail_ref[...]

        @pl.when((step > 0) & (step < blocks - 1))
        def _():
            num_ref[...] = sums_for(step * span, span)

    band_spec = pl.BlockSpec((rows_tile, RADIUS, width), lambda j: (0, 0, 0))
    return pl.pallas_call(
        kernel,
        grid=(blocks,),
        in_specs=[
            pl.BlockSpec((1, rows), lambda j: (0, 0)),
            pl.BlockSpec((rows, width), lambda j: (0, 0)),
            band_spec,
            band_spec,
        ],
        out_specs=pl.BlockSpec((rows_tile, span, width), lambda j: (0, j, 0)),
        out_shape=jax.ShapeDtypeStruct((rows_tile, cols_tile, width), jnp.float32),
    )(ids.reshape(1, rows), docs, lead, tail)


TAPS = [math.exp(-2.0 * k * k / RADIUS**2) for k in range(RADIUS + 1)]
GROUP = 4


def row_group(read, first, cols, lanes, emit):
    for c0 in range(0, cols, 8):
        window = [read(j, c0, lanes) for j in range(GROUP + 2 * RADIUS)]
        for q in range(GROUP):
            centre = q + RADIUS
            acc = TAPS[0] * window[centre]
            for k in range(1, RADIUS + 1):
                acc = acc + TAPS[k] * (window[centre - k] + window[centre + k])
            emit(first + q, c0, acc)


def updater(cb_ref, inv_ref, out_ref, lanes):
    def emit(r, c0, acc):
        base = cb_ref[r, pl.ds(c0, 8), lanes].astype(jnp.float32)
        upd = (acc + 8.0 * base) * inv_ref[r, pl.ds(c0, 8), :]
        out_ref[r, pl.ds(c0, 8), lanes] = upd.astype(out_ref.dtype)

    return emit


def inverter(inv_ref):
    def emit(r, c0, acc):
        inv_ref[r, pl.ds(c0, 8), :] = 1.0 / (acc[:, 2:3] + 8.0)

    return emit


def finish_inner(middle, codebook):
    rows, cols, feature = codebook.shape
    lanes = 128
    blocks = feature // lanes

    def kernel(mid_ref, cb_ref, out_ref, inv_ref):
        step = pl.program_id(0)

        def rows_pass(emit):
            def body(i, carry):
                first = RADIUS + i * GROUP

                def read(j, c0, part):
                    return mid_ref[first + j - RADIUS, pl.ds(c0, 8), part]

                row_group(read, first, cols, slice(None), emit)
                return carry

            lax.fori_loop(0, (rows - 2 * RADIUS) // GROUP, body, 0)

        @pl.when(step == 0)
        def _():
            rows_pass(inverter(inv_ref))

        @pl.when(step > 0)
        def _():
            rows_pass(updater(cb_ref, inv_ref, out_ref, slice(None)))

    out_spec = pl.BlockSpec((rows, cols, lanes), lambda j: (0, 0, jnp.maximum(j - 1, 0)))
    return pl.pallas_call(
        kernel,
        grid=(blocks + 1,),
        in_specs=[
            pl.BlockSpec((rows, cols, lanes), lambda j: (0, 0, (j + blocks) % (blocks + 1))),
            out_spec,
        ],
        out_specs=out_spec,
        out_shape=jax.ShapeDtypeStruct(codebook.shape, codebook.dtype),
        scratch_shapes=[pltpu.VMEM((rows, cols, 1), jnp.float32)],
    )(middle, codebook)


def finish_edges(above, middle, below, codebook, partial):
    rows, cols, feature = codebook.shape
    width = middle.shape[2]
    lanes = 128
    near = 2 * RADIUS
    last_edge = rows // RADIUS - 1

    def kernel(above_ref, mid_ref, below_ref, cb_ref, prev_ref, out_ref, ext_ref, inv_ref):
        del prev_ref
        side = pl.program_id(0)

        @pl.when(side == 0)
        def _():
            ext_ref[0:RADIUS] = above_ref[...]
            ext_ref[RADIUS:] = mid_ref[...]

        @pl.when(side == 1)
        def _():
            ext_ref[0:near] = mid_ref[...]
            ext_ref[near:] = below_ref[...]

        def body(i, carry):
            first = i * GROUP

            def read(j, c0, part):
                return ext_ref[first + j, pl.ds(c0, 8), part]

            row_group(read, first, cols, pl.ds(feature, lanes), inverter(inv_ref))
            for lane in range(0, feature, lanes):
                part = pl.ds(lane, lanes)
                row_group(read, first, cols, part, updater(cb_ref, inv_ref, out_ref, part))
            return carry

        lax.fori_loop(0, RADIUS // GROUP, body, 0)

    halo_spec = pl.BlockSpec((RADIUS, cols, width), lambda i: (0, 0, 0))
    edge_spec = pl.BlockSpec((RADIUS, cols, feature), lambda i: (i * last_edge, 0, 0))
    return pl.pallas_call(
        kernel,
        grid=(2,),
        in_specs=[
            halo_spec,
            pl.BlockSpec((near, cols, width), lambda i: (i * (rows // near - 1), 0, 0)),
            halo_spec,
            edge_spec,
            pl.BlockSpec(memory_space=pl.ANY),
        ],
        out_specs=edge_spec,
        out_shape=jax.ShapeDtypeStruct(codebook.shape, codebook.dtype),
        scratch_shapes=[
            pltpu.VMEM((near + RADIUS, cols, width), jnp.float32),
            pltpu.VMEM((RADIUS, cols, 1), jnp.float32),
        ],
        input_output_aliases={4: 0},
    )(above, middle, below, codebook, partial)


def exchange(lead, last, axis):
    devices = lax.axis_size(axis)
    up = [(i, i + 1) for i in range(devices - 1)]
    down = [(j, i) for i, j in up]
    return lax.ppermute(last, axis, up), lax.ppermute(lead, axis, down)


def on_device(documents, owner_tile, unit_in_tile, codebook):
    rows_mx = lax.axis_size("mx")
    cols_my = lax.axis_size("my")
    tile_total = rows_mx * cols_my
    rows_tile, cols_tile, feature = codebook.shape
    doc_count = documents.shape[0]
    capacity = max(2, 2 * doc_count // tile_total)
    target = owner_tile[:, 0]
    tile_hits = (target[:, None] == jnp.arange(tile_total, dtype=jnp.int32)[None, :]).astype(
        jnp.int32
    )
    earlier = jnp.cumsum(tile_hits, axis=0) - tile_hits
    slot_pos = jnp.sum(earlier * tile_hits, axis=1)
    unit_row = unit_in_tile // cols_tile
    unit_col = unit_in_tile % cols_tile
    extra = jnp.zeros((doc_count, 128), jnp.bfloat16)
    extra = extra.at[:, 0].set(unit_row.astype(jnp.bfloat16))
    extra = extra.at[:, 1].set(unit_col.astype(jnp.bfloat16))
    extra = extra.at[:, 2].set(1.0)
    rows_out = jnp.concatenate([documents, extra], axis=1)
    width = feature + 128
    send_place = target * capacity + slot_pos
    outgoing = jnp.zeros((tile_total * capacity, width), jnp.bfloat16).at[send_place].set(rows_out)
    got = lax.all_to_all(
        outgoing.reshape(tile_total, capacity, width),
        ("mx", "my"),
        split_axis=0,
        concat_axis=0,
        tiled=True,
    ).reshape(-1, width)
    mark_row = got[:, feature].astype(jnp.int32)
    mark_col = got[:, feature + 1].astype(jnp.int32)
    unit_ids = jnp.where(got[:, feature + 2] > 0.5, mark_row * cols_tile + mark_col, -1)
    col_total = cols_tile // RADIUS
    last = cols_tile - RADIUS
    lead, tail = accumulate_bands(unit_ids, got, rows_tile, cols_tile)
    from_left, from_right = exchange(lead, tail, "my")
    numerator = accumulate(unit_ids, got, rows_tile, cols_tile, lead, tail)

    g_rows = jnp.asarray(band_matrix(rows_tile))
    g_cols = jnp.asarray(band_matrix(cols_tile))
    last = rows_tile - RADIUS

    def col_pass(lo, hi):
        pieces = [from_left[lo:hi], numerator[lo:hi], from_right[lo:hi]]
        return jnp.einsum("ck,rke->rce", g_cols, jnp.concatenate(pieces, axis=1), precision=HI)

    col_top, col_bottom = col_pass(0, RADIUS), col_pass(last, rows_tile)

    above, below = exchange(col_top, col_bottom, "mx")
    col_num = col_pass(0, rows_tile)
    partial = finish_inner(col_num, codebook)
    return finish_edges(above, col_num, below, codebook, partial)


def solution(mesh):
    return jax.shard_map(
        on_device,
        mesh=mesh,
        in_specs=(
            P(("mx", "my"), None),
            P(("mx", "my"), None),
            P(("mx", "my")),
            P("mx", "my", None),
        ),
        out_specs=P("mx", "my", None),
        check_vma=False,
    )
```
